32 devices in a mesh: row: 8 (over z, y), col: 4 (over x, core).
Axes of the slice: x: 2, y: 2, z: 4, core: 2. Of those that a mesh axis runs over, the one named last changes fastest.
Arguments:
- inputs: bfloat16 [768, 16384], P('col', 'row'), may hold values from -6 to 6
- segments: int32 [8, 2048], P('row'), may hold values from 0 to 15, never falling along the last dimension, each value on 1 to 1024 neighbouring positions
- query_weight: bfloat16 [768, 768], P('row', 'col'), may hold values from -0.21875 to 0.21875
- key_weight: bfloat16 [768, 768], P('row', 'col'), may hold values from -0.21875 to 0.21875
- value_weight: bfloat16 [768, 768], P('row', 'col'), may hold values from -0.21875 to 0.21875
- query_bias: float32 [768], P('col'), may hold values from -3 to 3
- value_bias: float32 [768], P('col'), may hold values from -0.625 to 0.625
- output_weight: bfloat16 [768, 768], P('col', 'row'), may hold values from -1.75 to 1.75
- output_bias: float32 [768], P('col'), may hold values from -1.75 to 1.75
- attn_gain: float32 [768], P('col'), may hold values from 0.5 to 1.5
- attn_shift: float32 [768], P('col'), may hold values from -1.75 to 1.75
- up_weight: bfloat16 [768, 3072], P('row', 'col'), may hold values from -0.21875 to 0.21875
- up_bias: float32 [3072], P('col'), may hold values from -3 to 3
- down_weight: bfloat16 [3072, 768], P('col', 'row'), may hold values from -0.109375 to 0.109375
- down_bias: float32 [768], P('col'), may hold values from -1.75 to 1.75
- final_gain: float32 [768], P('col'), may hold values from 0.5 to 1.5
- final_shift: float32 [768], P('col'), may hold values from -1.75 to 1.75
- cotangent: bfloat16 [768, 16384], P('col', 'row'), may hold values from -6 to 6
Outputs:
- layer_out: bfloat16 [768, 16384], P('col', 'row')
- input_grad: bfloat16 [768, 16384], P('col', 'row')
- query_weight_grad: float32 [768, 768], P('row', 'col')
- key_weight_grad: float32 [768, 768], P('row', 'col')
- value_weight_grad: float32 [768, 768], P('row', 'col')
- query_bias_grad: float32 [768], P('col')
- value_bias_grad: float32 [768], P('col')
- output_weight_grad: float32 [768, 768], P('col', 'row')
- output_bias_grad: float32 [768], P('col')
- attn_gain_grad: float32 [768], P('col')
- attn_shift_grad: float32 [768], P('col')
- up_weight_grad: float32 [768, 3072], P('row', 'col')
- up_bias_grad: float32 [3072], P('col')
- down_weight_grad: float32 [3072, 768], P('col', 'row')
- down_bias_grad: float32 [768], P('col')
- final_gain_grad: float32 [768], P('col')
- final_shift_grad: float32 [768], P('col')
The draws below stay inside these ranges and needn't reach their ends.
Inputs may be any that keep to these rules, and one draw needn't show every extreme that they name: `segments`: along each sequence of 2048 tokens the numbers never fall; 0 marks padding tokens; one number covers at most 1024 tokens of a sequence.
All inputs are finite; a program needn't handle non-finite values.
Results may differ from the reference program's by a relative error of at most 0.015.
Values may be sent and summed in bfloat16 or wider, within the bound.
No kernel may reach another device: no remote copies, remote signals or barrier semaphores. Data moves between devices by JAX's collectives and lax.ppermute only.
A program may use at most 256 MiB of HBM per device.

```python
import math
import jax
import jax.numpy as jnp
import numpy as np
from jax import lax

D = 768
HEADS = 12
FF = 3072
SEQ = 2048
SEGS = 16
TOKENS = 16384
N_ROW = 8


def strengthened(values, key, source, target, shards_of, factor):
    def block_of(position):
        return (jnp.arange(values.shape[position]) // (values.shape[position] // shards_of)).reshape((-1,) + (1,) * (values.ndim - 1 - position))

    one_side = jax.random.permutation(key, shards_of)[block_of(target)]
    other_side = (block_of(target) + shards_of // 2) % shards_of
    return jnp.where((block_of(source) == one_side) | (block_of(source) == other_side), factor * values, values)


def block_scale(key, shape, pieces, least, top_value):
    factor_of, own = 1.0, jax.random.fold_in(key, 6)
    for position, parts in pieces:
        steps = jnp.exp(jax.random.uniform(jax.random.fold_in(own, position), (parts,), jnp.float32, least / len(pieces), top_value / len(pieces)))
        factor_of = factor_of * jnp.repeat(steps, shape[position] // parts).reshape([-1 if axis == position else 1 for axis in range(len(shape))])
    return factor_of


def profile(number_of, total, bound, skew):
    loads = [(1 << 20) // math.isqrt(grade ** skew) + 1 for grade in range(2, number_of + 1)]
    spare, given = total - bound - (number_of - 1), [1] * (number_of - 1)
    while spare > 0:
        free = [i for i in range(number_of - 1) if given[i] < bound]
        pool, remaining = sum([loads[i] for i in free]), spare
        for i in free:
            extra = min(bound - given[i], max(1, remaining * loads[i] // pool), spare)
            given[i] = given[i] + extra
            spare = spare - extra
    return np.array([bound] + given)


def ragged_sizes(stream_key, number_of, total, limit, lean):
    if number_of == 2:
        one = jax.random.randint(stream_key, (), max(1, total - limit), min(limit, total - 1) + 1)
        return jnp.stack([one, total - one])
    tallies = jnp.asarray(profile(number_of, total, limit, lean), jnp.int32)
    twos = (number_of - 1) // 2
    giver, sink = tallies[1:1 + 2 * twos:2], tallies[2:2 + 2 * twos:2]
    room = jnp.minimum(giver - 1, limit - sink)
    moved = jax.random.randint(jax.random.fold_in(stream_key, 1), (twos,), 0, 1 << 20) % (room + 1)
    tallies = tallies.at[1:1 + 2 * twos:2].set(giver - moved).at[2:2 + 2 * twos:2].set(sink + moved)
    return tallies[jax.random.permutation(jax.random.fold_in(stream_key, 2), number_of)]


def gaussian(stream_key, shape, spread, most, shards=(), dtype=jnp.bfloat16):
    values = jax.random.normal(stream_key, shape, jnp.float32) * spread
    if len(shards) > 0:
        values = block_scale(stream_key, shape, shards, -0.22, 0.18) * values
    return jnp.clip(values, min=-most, max=most).astype(dtype)


def noise_with(stream_key, shape, scale, limit, split, heavy, dtype=jnp.bfloat16):
    drawn = scale * jax.random.normal(stream_key, shape, jnp.float32)
    if split:
        drawn = drawn * block_scale(stream_key, shape, split, -0.22, 0.18)
    return jnp.clip(strengthened(drawn, jax.random.fold_in(stream_key, 3), *heavy), -limit, limit).astype(dtype)


def setup_inputs(seed: int = 0) -> dict:
    streams_of = jax.random.split(jax.random.key(seed), 19)
    return {
        "inputs": noise_with(streams_of[0], (D, TOKENS), 1.0, 6.0, ((0, 4), (1, 8)), (1, 0, 8, 2.0)),
        "segments": jax.vmap(lambda own: jnp.searchsorted(jnp.cumsum(ragged_sizes(own, SEGS, SEQ, SEQ // 2, 2)), jnp.arange(SEQ), side="right"))(jax.random.split(streams_of[1], N_ROW)).reshape((N_ROW, SEQ)).astype(jnp.int32),
        "query_weight": gaussian(streams_of[2], (D, D), D ** -0.5, 0.21875, ((0, 8), (1, 4))),
        "key_weight": gaussian(streams_of[3], (D, D), D ** -0.5, 0.21875, ((0, 8), (1, 4))),
        "value_weight": gaussian(streams_of[4], (D, D), D ** -0.5, 0.21875, ((0, 8), (1, 4))),
        "query_bias": gaussian(streams_of[5], (D,), 0.5, 3.0, ((0, 4),), jnp.float32),
        "value_bias": gaussian(streams_of[6], (D,), 0.1, 0.625, ((0, 4),), jnp.float32),
        "output_weight": gaussian(streams_of[7], (D, D), (D // min(64, max(1, SEQ // SEGS))) ** -0.5, 1.75, ((0, 4), (1, 8))),
        "output_bias": gaussian(streams_of[8], (D,), 0.3, 1.75, ((0, 4),), jnp.float32),
        "attn_gain": jnp.clip(1.0 + 0.1 * jax.random.normal(streams_of[9], (D,), jnp.float32), 0.5, 1.5),
        "attn_shift": gaussian(streams_of[10], (D,), 0.3, 1.75, ((0, 4),), jnp.float32),
        "up_weight": gaussian(streams_of[11], (D, FF), D ** -0.5, 0.21875, ((0, 8), (1, 4))),
        "up_bias": gaussian(streams_of[12], (FF,), 0.5, 3.0, ((0, 4),), jnp.float32),
        "down_weight": gaussian(streams_of[13], (FF, D), FF ** -0.5, 0.109375, ((0, 4), (1, 8))),
        "down_bias": gaussian(streams_of[14], (D,), 0.3, 1.75, ((0, 4),), jnp.float32),
        "final_gain": jnp.clip(1.0 + 0.1 * jax.random.normal(streams_of[15], (D,), jnp.float32), 0.5, 1.5),
        "final_shift": gaussian(streams_of[16], (D,), 0.3, 1.75, ((0, 4),), jnp.float32),
        "cotangent": noise_with(streams_of[17], (D, TOKENS), 1.0, 6.0, ((0, 4), (1, 8)), (1, 0, 8, 2.0)),
    }


@jax.custom_vjp
def low(v):
    return lax.optimization_barrier(v.astype(jnp.bfloat16)).astype(jnp.float32)

@jax.custom_vjp
def low_back(v):
    return v

def low_keep(v):
    return (low(v), None)

def low_pass(kept, grad):
    return (grad,)

def back_keep(v):
    return (v, None)

def back_low(kept, grad):
    return (low(grad),)
low.defvjp(low_keep, low_pass)
low_back.defvjp(back_keep, back_low)

def matmul(left, right):
    return jnp.dot(left, right, precision=lax.Precision.HIGHEST, preferred_element_type=jnp.float32)

def normalize(row_values, gain_row, shift_row):
    mean_row = lax.optimization_barrier(jnp.mean(row_values, axis=-1, keepdims=True))
    square_row = lax.optimization_barrier(jnp.mean(row_values * row_values, axis=-1, keepdims=True))
    normed = (row_values - mean_row) * lax.rsqrt(square_row - mean_row * mean_row + 1e-06)
    return normed * gain_row + shift_row

def attend_one(packed):
    queries, key_all, value_all, labels = packed
    score_scale = queries.shape[-1] ** (-0.5)
    scores = low_back(score_scale * jnp.einsum('qhd,khd->hqk', queries, key_all, precision=lax.Precision.HIGHEST))
    places = jnp.arange(labels.shape[0])
    allowed = (labels[:, None] == labels[None, :]) & (labels[None, :] > 0) | (places[:, None] == places[None, :])
    scores = jnp.where(allowed[None], scores, -1000000000.0)
    highest = lax.optimization_barrier(jnp.max(scores, axis=-1, keepdims=True))
    exponent = jnp.exp(scores - highest)
    probability = exponent / lax.optimization_barrier(jnp.sum(exponent, axis=-1, keepdims=True))
    return jnp.einsum('hqk,khd->qhd', low(probability), value_all, precision=lax.Precision.HIGHEST)

def reference(inputs, segments, query_weight, key_weight, value_weight, query_bias, value_bias, output_weight, output_bias, attn_gain, attn_shift, up_weight, up_bias, down_weight, down_bias, final_gain, final_shift, cotangent):
    head_size = D // HEADS

    def forward(inputs, query_weight, key_weight, value_weight, query_bias, value_bias, output_weight, output_bias, attn_gain, attn_shift, up_weight, up_bias, down_weight, down_bias, final_gain, final_shift):
        row_count = inputs.shape[0]

        def heads_view(matrix):
            return matrix.reshape(row_count // SEQ, SEQ, HEADS, head_size)
        queries = low_back(low(matmul(inputs, query_weight) + query_bias))
        key_all = low_back(low(matmul(inputs, key_weight)))
        value_all = low_back(low(matmul(inputs, value_weight) + value_bias))
        attended = lax.map(jax.checkpoint(attend_one), (heads_view(queries), heads_view(key_all), heads_view(value_all), segments))
        attended = low_back(low(attended.reshape(row_count, D)))
        attn_branch = low_back(matmul(attended, output_weight) + output_bias)
        hidden = normalize(inputs + attn_branch, attn_gain, attn_shift)
        upped = low_back(matmul(low(hidden), up_weight) + up_bias)
        acted = low(jax.nn.gelu(upped, approximate=False))
        ffn_branch = low_back(matmul(acted, down_weight) + down_bias)
        return normalize(hidden + ffn_branch, final_gain, final_shift)
    arrays = tuple((argument.astype(jnp.float32) for argument in (inputs.T, query_weight, key_weight, value_weight, query_bias, value_bias, output_weight, output_bias, attn_gain, attn_shift, up_weight, up_bias, down_weight, down_bias, final_gain, final_shift)))
    layer_out, pull_back = jax.vjp(forward, *arrays)
    grads = pull_back(cotangent.T.astype(jnp.float32))
    return (layer_out.T.astype(jnp.bfloat16), grads[0].T.astype(jnp.bfloat16), grads[1], grads[2], grads[3], grads[4], grads[5], grads[6], grads[7], grads[8], grads[9], grads[10], grads[11], grads[12], grads[13], grads[14], grads[15])
```

```python
from functools import partial
import functools

import jax
import jax.numpy as jnp
from jax import lax
from jax.experimental import pallas as pl
from jax.experimental.pallas import tpu as pltpu
from jax.sharding import PartitionSpec as P

D = 768
HEADS = 12
BQ = 256


def _mask(lab_q, lab_k, q0, bq, nk):
    rows = q0 + lax.broadcasted_iota(jnp.int32, (bq, nk), 0)
    cols = lax.broadcasted_iota(jnp.int32, (bq, nk), 1)
    return ((lab_q == lab_k) & (lab_k > 0)) | (rows == cols)


def _fwd_kernel(scale, q_ref, k_ref, v_ref, lq_ref, lk_ref, o_ref, m_ref, l_ref):
    i = pl.program_id(1)
    bq = q_ref.shape[0]
    nk = k_ref.shape[0]
    s = lax.dot_general(q_ref[...], k_ref[...], (((1,), (1,)), ((), ())),
                        preferred_element_type=jnp.float32) * scale
    allowed = _mask(lq_ref[...], lk_ref[...], i * bq, bq, nk)
    s = jnp.where(allowed, s, -1000000000.0)
    m = jnp.max(s, axis=1, keepdims=True)
    e = jnp.exp(s - m)
    l = jnp.sum(e, axis=1, keepdims=True)
    p = (e / l).astype(jnp.bfloat16)
    o_ref[...] = jnp.dot(p, v_ref[...], preferred_element_type=jnp.float32).astype(o_ref.dtype)
    m_ref[...] = m
    l_ref[...] = l


def _bwd_kernel(scale, q_ref, k_ref, v_ref, do_ref, lq_ref, lk_ref, m_ref, l_ref,
                dq_ref, dk_ref, dv_ref):
    i = pl.program_id(1)
    bq = q_ref.shape[0]
    nk = k_ref.shape[0]

    @pl.when(i == 0)
    def _():
        dk_ref[...] = jnp.zeros_like(dk_ref)
        dv_ref[...] = jnp.zeros_like(dv_ref)

    q = q_ref[...]
    k = k_ref[...]
    s = lax.dot_general(q, k, (((1,), (1,)), ((), ())),
                        preferred_element_type=jnp.float32) * scale
    allowed = _mask(lq_ref[...], lk_ref[...], i * bq, bq, nk)
    s = jnp.where(allowed, s, -1000000000.0)
    p = jnp.where(allowed, jnp.exp(s - m_ref[...]) / l_ref[...], 0.0)
    do = do_ref[...]
    dp = lax.dot_general(do, v_ref[...], (((1,), (1,)), ((), ())),
                         preferred_element_type=jnp.float32)
    inner = jnp.sum(p * dp, axis=1, keepdims=True)
    ds = (p * (dp - inner)).astype(jnp.bfloat16)
    dq_ref[...] = (jnp.dot(ds, k, preferred_element_type=jnp.float32) * scale).astype(dq_ref.dtype)
    dk_ref[...] += lax.dot_general(ds, q, (((0,), (0,)), ((), ())),
                                   preferred_element_type=jnp.float32) * scale
    dv_ref[...] += lax.dot_general(p.astype(jnp.bfloat16), do, (((0,), (0,)), ((), ())),
                                   preferred_element_type=jnp.float32)


def attention_forward(q, k, v, labels, scale):
    nh, seq, hd = q.shape
    bq = min(BQ, seq)
    lq = labels.reshape(seq, 1)
    lk = labels.reshape(1, seq)
    grid = (nh, seq // bq)
    qspec = pl.BlockSpec((None, bq, hd), lambda h, i: (h, i, 0))
    kspec = pl.BlockSpec((None, seq, hd), lambda h, i: (h, 0, 0))
    rowspec = pl.BlockSpec((None, bq, 1), lambda h, i: (h, i, 0))
    flops = 4 * nh * seq * seq * hd
    return pl.pallas_call(
        functools.partial(_fwd_kernel, scale),
        grid=grid,
        in_specs=[qspec, kspec, kspec,
                  pl.BlockSpec((bq, 1), lambda h, i: (i, 0)),
                  pl.BlockSpec((1, seq), lambda h, i: (0, 0))],
        out_specs=[qspec, rowspec, rowspec],
        out_shape=[jax.ShapeDtypeStruct((nh, seq, hd), jnp.bfloat16),
                   jax.ShapeDtypeStruct((nh, seq, 1), jnp.float32),
                   jax.ShapeDtypeStruct((nh, seq, 1), jnp.float32)],
        compiler_params=pltpu.CompilerParams(
            dimension_semantics=("parallel", "arbitrary"),
            vmem_limit_bytes=48 * 1024 * 1024),
        cost_estimate=pl.CostEstimate(flops=flops, transcendentals=nh * seq * seq,
                                      bytes_accessed=4 * nh * seq * hd * 2),
    )(q, k, v, lq, lk)


def attention_backward(q, k, v, do, labels, m, l, scale):
    nh, seq, hd = q.shape
    bq = min(BQ, seq)
    lq = labels.reshape(seq, 1)
    lk = labels.reshape(1, seq)
    grid = (nh, seq // bq)
    qspec = pl.BlockSpec((None, bq, hd), lambda h, i: (h, i, 0))
    kspec = pl.BlockSpec((None, seq, hd), lambda h, i: (h, 0, 0))
    rowspec = pl.BlockSpec((None, bq, 1), lambda h, i: (h, i, 0))
    flops = 10 * nh * seq * seq * hd
    return pl.pallas_call(
        functools.partial(_bwd_kernel, scale),
        grid=grid,
        in_specs=[qspec, kspec, kspec, qspec,
                  pl.BlockSpec((bq, 1), lambda h, i: (i, 0)),
                  pl.BlockSpec((1, seq), lambda h, i: (0, 0)),
                  rowspec, rowspec],
        out_specs=[qspec, kspec, kspec],
        out_shape=[jax.ShapeDtypeStruct((nh, seq, hd), jnp.bfloat16),
                   jax.ShapeDtypeStruct((nh, seq, hd), jnp.float32),
                   jax.ShapeDtypeStruct((nh, seq, hd), jnp.float32)],
        compiler_params=pltpu.CompilerParams(
            dimension_semantics=("parallel", "arbitrary"),
            vmem_limit_bytes=48 * 1024 * 1024),
        cost_estimate=pl.CostEstimate(flops=flops, transcendentals=nh * seq * seq,
                                      bytes_accessed=8 * nh * seq * hd * 2),
    )(q, k, v, do, lq, lk, m, l)


NORM_EPS = 1e-06


def feature_whole(blocked):
    return lax.all_gather(blocked, "col", axis=1, tiled=True)


def feature_sum(partial_rows):
    return lax.psum_scatter(partial_rows, "col", scatter_dimension=1, tiled=True)


def row_totals(first_term, second_term):
    return lax.psum((jnp.sum(first_term, axis=1), jnp.sum(second_term, axis=1)), "col")


def norm_forward(row_values, gain_row, shift_row):
    totals, squares = row_totals(row_values, row_values * row_values)
    mean_row = (totals / D)[:, None]
    var_row = (squares / D)[:, None] - mean_row * mean_row
    inverse = lax.rsqrt(var_row + NORM_EPS)
    normed = (row_values - mean_row) * inverse
    return (normed * gain_row + shift_row, normed, inverse)


def norm_backward(grad_rows, normed, inverse, gain_row):
    scaled = grad_rows * gain_row
    totals, along = row_totals(scaled, scaled * normed)
    back_rows = inverse * (scaled - (totals / D)[:, None] - normed * (along / D)[:, None])
    return (back_rows, jnp.sum(grad_rows * normed, axis=0), jnp.sum(grad_rows, axis=0))


def project_in(gathered, stacked):
    complete = lax.all_gather(stacked, "row", axis=1, tiled=True)
    return (
        jnp.einsum("td,kdc->ktc", gathered, complete, preferred_element_type=jnp.float32),
        complete,
    )


def project_in_back(grad_stack, stacked, complete):
    complete = lax.all_gather(stacked, "row", axis=1, tiled=True)
    return jnp.einsum("ktc,kdc->td", grad_stack, complete, preferred_element_type=jnp.float32)


def columns_whole(weight_block):
    return lax.all_gather(weight_block, "row", axis=1, tiled=True)


def project_out_back(grad_full, weight_block, complete):
    contract = (((1,), (1,)), ((), ()))
    complete = lax.all_gather(weight_block, "row", axis=1, tiled=True)
    return lax.dot_general(grad_full, complete, contract, preferred_element_type=jnp.float32)


def weight_grad(gathered, local_grad):
    own_rows = gathered.shape[1] // lax.axis_size("row")
    columns = lax.slice_in_dim(gathered, 0, lax.axis_size("row") * own_rows, axis=1)
    return lax.psum_scatter(
        lax.dot_general(
            columns, local_grad, (((0,), (0,)), ((), ())), preferred_element_type=jnp.float32
        ),
        "row",
        scatter_dimension=0,
        tiled=True,
    )


def heads_major(rows, head_size):
    return rows.reshape(rows.shape[0], -1, head_size).transpose(1, 0, 2)


def heads_beside(stacked):
    return stacked.transpose(1, 0, 2).reshape(stacked.shape[1], -1)


def full_norm(row_values, gain_full, shift_full):
    mean_row = jnp.sum(row_values, axis=1, keepdims=True) / D
    var_row = jnp.sum(row_values * row_values, axis=1, keepdims=True) / D - mean_row * mean_row
    inverse = lax.rsqrt(var_row + NORM_EPS)
    normed = (row_values - mean_row) * inverse
    return (normed * gain_full + shift_full, normed, inverse)


def body(
    inputs,
    segments,
    query_weight,
    key_weight,
    value_weight,
    query_bias,
    value_bias,
    output_weight,
    output_bias,
    attn_gain,
    attn_shift,
    up_weight,
    up_bias,
    down_weight,
    down_bias,
    final_gain,
    final_shift,
    cotangent,
):
    head_size = D // HEADS
    score_scale = head_size ** (-0.5)
    labels = segments[0]
    token_rows = inputs.T
    out_grad = cotangent.T.astype(jnp.float32)
    token_count = token_rows.shape[0]
    own_features = token_rows.shape[1]
    own_start = lax.axis_index("col") * own_features
    inputs_full = feature_whole(token_rows)
    qkv_stack = jnp.stack([query_weight, key_weight, value_weight])
    projected, qkv_complete = project_in(inputs_full, qkv_stack)
    queries = heads_major((projected[0] + query_bias).astype(jnp.bfloat16), head_size)
    key_all = heads_major(projected[1].astype(jnp.bfloat16), head_size)
    value_all = heads_major((projected[2] + value_bias).astype(jnp.bfloat16), head_size)
    attended_h, row_max, row_total = attention_forward(
        queries, key_all, value_all, labels, score_scale
    )
    attended = heads_beside(attended_h)
    attended_full = feature_whole(attended)
    output_rows = columns_whole(output_weight)
    output_complete = lax.all_gather(output_rows, "col", axis=0, tiled=True)
    output_bias_full = lax.all_gather(output_bias, "col", axis=0, tiled=True)
    gain_one_full = lax.all_gather(attn_gain, "col", axis=0, tiled=True)
    shift_one_full = lax.all_gather(attn_shift, "col", axis=0, tiled=True)
    first_sum_full = (
        inputs_full.astype(jnp.float32)
        + jnp.dot(attended_full, output_complete, preferred_element_type=jnp.float32)
        + output_bias_full
    )
    hidden_full_f, normed_one_full, inverse_one = full_norm(
        first_sum_full, gain_one_full, shift_one_full
    )
    hidden = lax.dynamic_slice_in_dim(hidden_full_f, own_start, own_features, axis=1)
    normed_one = lax.dynamic_slice_in_dim(normed_one_full, own_start, own_features, axis=1)
    hidden_full = hidden_full_f.astype(jnp.bfloat16)
    up_stack = up_weight[None]
    up_projected, up_complete = project_in(hidden_full, up_stack)
    upped = up_projected[0] + up_bias
    acted_f, gelu_pull = jax.vjp(partial(jax.nn.gelu, approximate=False), upped)
    acted = acted_f.astype(jnp.bfloat16)
    down_complete = columns_whole(down_weight)
    ffn_partial = jnp.dot(acted, down_complete, preferred_element_type=jnp.float32)
    second_sum = hidden + feature_sum(ffn_partial) + down_bias
    result, normed_two, inverse_two = norm_forward(second_sum, final_gain, final_shift)
    second_grad, final_gain_grad, final_shift_grad = norm_backward(
        out_grad, normed_two, inverse_two, final_gain
    )
    branch_grad = second_grad.astype(jnp.bfloat16)
    branch_full = feature_whole(branch_grad)
    down_weight_grad = weight_grad(branch_full, acted).T
    acted_grad = project_out_back(branch_full, down_weight, down_complete)
    upped_grad = gelu_pull(acted_grad)[0].astype(jnp.bfloat16)
    up_weight_grad = weight_grad(hidden_full, upped_grad)
    hidden_grad = second_grad + feature_sum(
        project_in_back(upped_grad[None], up_stack, up_complete)
    )
    first_grad, attn_gain_grad, attn_shift_grad = norm_backward(
        hidden_grad, normed_one, inverse_one, attn_gain
    )
    attn_branch_grad = first_grad.astype(jnp.bfloat16)
    attn_branch_full = feature_whole(attn_branch_grad)
    output_weight_grad = weight_grad(attn_branch_full, attended).T
    attended_grad = project_out_back(attn_branch_full, output_weight, output_rows).astype(
        jnp.bfloat16
    )
    query_grad_h, key_grad_h, value_grad_h = attention_backward(
        queries,
        key_all,
        value_all,
        heads_major(attended_grad, head_size),
        labels,
        row_max,
        row_total,
        score_scale,
    )
    query_grad = heads_beside(query_grad_h)
    key_grad = heads_beside(key_grad_h).astype(jnp.bfloat16)
    value_grad = heads_beside(value_grad_h).astype(jnp.bfloat16)
    column_count = query_weight.shape[1]
    qkv_grads = weight_grad(
        inputs_full, jnp.concatenate([query_grad, key_grad, value_grad], axis=1)
    )
    input_grad = first_grad + feature_sum(
        project_in_back(jnp.stack([query_grad, key_grad, value_grad]), qkv_stack, qkv_complete)
    )
    param_totals = lax.psum(
        (
            jnp.sum(query_grad.astype(jnp.float32), axis=0),
            jnp.sum(value_grad.astype(jnp.float32), axis=0),
            jnp.sum(attn_branch_grad.astype(jnp.float32), axis=0),
            attn_gain_grad,
            attn_shift_grad,
            jnp.sum(upped_grad.astype(jnp.float32), axis=0),
            jnp.sum(branch_grad.astype(jnp.float32), axis=0),
            final_gain_grad,
            final_shift_grad,
        ),
        "row",
    )
    return (
        result.astype(jnp.bfloat16).T,
        input_grad.astype(jnp.bfloat16).T,
        qkv_grads[:, :column_count],
        qkv_grads[:, column_count : 2 * column_count],
        qkv_grads[:, 2 * column_count :],
        param_totals[0],
        param_totals[1],
        output_weight_grad,
        param_totals[2],
        param_totals[3],
        param_totals[4],
        up_weight_grad,
        param_totals[5],
        down_weight_grad,
        param_totals[6],
        param_totals[7],
        param_totals[8],
    )


def solution(mesh):
    placed = (
        P("col", "row"),
        P("row", None),
        P("row", "col"),
        P("row", "col"),
        P("row", "col"),
        P("col"),
        P("col"),
        P("col", "row"),
        P("col"),
        P("col"),
        P("col"),
        P("row", "col"),
        P("col"),
        P("col", "row"),
        P("col"),
        P("col"),
        P("col"),
        P("col", "row"),
    )
    return jax.shard_map(
        body,
        mesh=mesh,
        in_specs=placed,
        out_specs=(
            P("col", "row"),
            P("col", "row"),
            P("row", "col"),
            P("row", "col"),
            P("row", "col"),
            P("col"),
            P("col"),
            P("col", "row"),
            P("col"),
            P("col"),
            P("col"),
            P("row", "col"),
            P("col"),
            P("col", "row"),
            P("col"),
            P("col"),
            P("col"),
        ),
        check_vma=False,
    )
```

```python
from functools import partial
import functools

import jax
import jax.numpy as jnp
from jax import lax
from jax.experimental import pallas as pl
from jax.experimental.pallas import tpu as pltpu
from jax.sharding import PartitionSpec as P

D = 768
HEADS = 12
BQ = 256


def _mask(lab_q, lab_k, q0, bq, nk):
    rows = q0 + lax.broadcasted_iota(jnp.int32, (bq, nk), 0)
    cols = lax.broadcasted_iota(jnp.int32, (bq, nk), 1)
    return ((lab_q == lab_k) & (lab_k > 0)) | (rows == cols)


def _fwd_kernel(scale, q_ref, k_ref, v_ref, lq_ref, lk_ref, o_ref, m_ref, l_ref):
    i = pl.program_id(1)
    bq = q_ref.shape[0]
    nk = k_ref.shape[0]
    s = lax.dot_general(q_ref[...], k_ref[...], (((1,), (1,)), ((), ())),
                        preferred_element_type=jnp.float32) * scale
    allowed = _mask(lq_ref[...], lk_ref[...], i * bq, bq, nk)
    s = jnp.where(allowed, s, -1000000000.0)
    m = jnp.max(s, axis=1, keepdims=True)
    e = jnp.exp(s - m)
    l = jnp.sum(e, axis=1, keepdims=True)
    p = (e / l).astype(jnp.bfloat16)
    o_ref[...] = jnp.dot(p, v_ref[...], preferred_element_type=jnp.float32).astype(o_ref.dtype)
    m_ref[...] = m
    l_ref[...] = l


def _bwd_kernel(scale, q_ref, k_ref, v_ref, do_ref, lq_ref, lk_ref, m_ref, l_ref,
                dq_ref, dk_ref, dv_ref):
    i = pl.program_id(1)
    bq = q_ref.shape[0]
    nk = k_ref.shape[0]

    @pl.when(i == 0)
    def _():
        dk_ref[...] = jnp.zeros_like(dk_ref)
        dv_ref[...] = jnp.zeros_like(dv_ref)

    q = q_ref[...]
    k = k_ref[...]
    s = lax.dot_general(q, k, (((1,), (1,)), ((), ())),
                        preferred_element_type=jnp.float32) * scale
    allowed = _mask(lq_ref[...], lk_ref[...], i * bq, bq, nk)
    s = jnp.where(allowed, s, -1000000000.0)
    p = jnp.where(allowed, jnp.exp(s - m_ref[...]) / l_ref[...], 0.0)
    do = do_ref[...]
    dp = lax.dot_general(do, v_ref[...], (((1,), (1,)), ((), ())),
                         preferred_element_type=jnp.float32)
    inner = jnp.sum(p * dp, axis=1, keepdims=True)
    ds = (p * (dp - inner)).astype(jnp.bfloat16)
    dq_ref[...] = (jnp.dot(ds, k, preferred_element_type=jnp.float32) * scale).astype(dq_ref.dtype)
    dk_ref[...] += lax.dot_general(ds, q, (((0,), (0,)), ((), ())),
                                   preferred_element_type=jnp.float32) * scale
    dv_ref[...] += lax.dot_general(p.astype(jnp.bfloat16), do, (((0,), (0,)), ((), ())),
                                   preferred_element_type=jnp.float32)


def attention_forward(q, k, v, labels, scale):
    nh, seq, hd = q.shape
    bq = min(BQ, seq)
    lq = labels.reshape(seq, 1)
    lk = labels.reshape(1, seq)
    grid = (nh, seq // bq)
    qspec = pl.BlockSpec((None, bq, hd), lambda h, i: (h, i, 0))
    kspec = pl.BlockSpec((None, seq, hd), lambda h, i: (h, 0, 0))
    rowspec = pl.BlockSpec((None, bq, 1), lambda h, i: (h, i, 0))
    flops = 4 * nh * seq * seq * hd
    return pl.pallas_call(
        functools.partial(_fwd_kernel, scale),
        grid=grid,
        in_specs=[qspec, kspec, kspec,
                  pl.BlockSpec((bq, 1), lambda h, i: (i, 0)),
                  pl.BlockSpec((1, seq), lambda h, i: (0, 0))],
        out_specs=[qspec, rowspec, rowspec],
        out_shape=[jax.ShapeDtypeStruct((nh, seq, hd), jnp.bfloat16),
                   jax.ShapeDtypeStruct((nh, seq, 1), jnp.float32),
                   jax.ShapeDtypeStruct((nh, seq, 1), jnp.float32)],
        compiler_params=pltpu.CompilerParams(
            dimension_semantics=("parallel", "arbitrary"),
            vmem_limit_bytes=48 * 1024 * 1024),
        cost_estimate=pl.CostEstimate(flops=flops, transcendentals=nh * seq * seq,
                                      bytes_accessed=4 * nh * seq * hd * 2),
    )(q, k, v, lq, lk)


def attention_backward(q, k, v, do, labels, m, l, scale):
    nh, seq, hd = q.shape
    bq = min(BQ, seq)
    lq = labels.reshape(seq, 1)
    lk = labels.reshape(1, seq)
    grid = (nh, seq // bq)
    qspec = pl.BlockSpec((None, bq, hd), lambda h, i: (h, i, 0))
    kspec = pl.BlockSpec((None, seq, hd), lambda h, i: (h, 0, 0))
    rowspec = pl.BlockSpec((None, bq, 1), lambda h, i: (h, i, 0))
    flops = 10 * nh * seq * seq * hd
    return pl.pallas_call(
        functools.partial(_bwd_kernel, scale),
        grid=grid,
        in_specs=[qspec, kspec, kspec, qspec,
                  pl.BlockSpec((bq, 1), lambda h, i: (i, 0)),
                  pl.BlockSpec((1, seq), lambda h, i: (0, 0)),
                  rowspec, rowspec],
        out_specs=[qspec, kspec, kspec],
        out_shape=[jax.ShapeDtypeStruct((nh, seq, hd), jnp.bfloat16),
                   jax.ShapeDtypeStruct((nh, seq, hd), jnp.float32),
                   jax.ShapeDtypeStruct((nh, seq, hd), jnp.float32)],
        compiler_params=pltpu.CompilerParams(
            dimension_semantics=("parallel", "arbitrary"),
            vmem_limit_bytes=48 * 1024 * 1024),
        cost_estimate=pl.CostEstimate(flops=flops, transcendentals=nh * seq * seq,
                                      bytes_accessed=8 * nh * seq * hd * 2),
    )(q, k, v, do, lq, lk, m, l)


NORM_EPS = 1e-06


def feature_whole(blocked):
    return lax.all_gather(blocked, "col", axis=1, tiled=True)


def feature_sum(partial_rows):
    return lax.psum_scatter(partial_rows, "col", scatter_dimension=1, tiled=True)


def row_totals(first_term, second_term):
    return lax.psum((jnp.sum(first_term, axis=1), jnp.sum(second_term, axis=1)), "col")


def norm_forward(row_values, gain_row, shift_row):
    totals, squares = row_totals(row_values, row_values * row_values)
    mean_row = (totals / D)[:, None]
    var_row = (squares / D)[:, None] - mean_row * mean_row
    inverse = lax.rsqrt(var_row + NORM_EPS)
    normed = (row_values - mean_row) * inverse
    return (normed * gain_row + shift_row, normed, inverse)


def norm_backward(grad_rows, normed, inverse, gain_row):
    scaled = grad_rows * gain_row
    totals, along = row_totals(scaled, scaled * normed)
    back_rows = inverse * (scaled - (totals / D)[:, None] - normed * (along / D)[:, None])
    return (back_rows, jnp.sum(grad_rows * normed, axis=0), jnp.sum(grad_rows, axis=0))


def project_in(gathered, stacked):
    complete = lax.all_gather(stacked, "row", axis=1, tiled=True)
    return (
        jnp.einsum("td,kdc->ktc", gathered, complete, preferred_element_type=jnp.float32),
        complete,
    )


def project_in_back(grad_stack, stacked, complete):
    complete = lax.all_gather(stacked, "row", axis=1, tiled=True)
    return jnp.einsum("ktc,kdc->td", grad_stack, complete, preferred_element_type=jnp.float32)


def columns_whole(weight_block):
    return lax.all_gather(weight_block, "row", axis=1, tiled=True)


def project_out_back(grad_full, weight_block, complete):
    contract = (((1,), (1,)), ((), ()))
    complete = lax.all_gather(weight_block, "row", axis=1, tiled=True)
    return lax.dot_general(grad_full, complete, contract, preferred_element_type=jnp.float32)


def weight_grad(gathered, local_grad):
    own_rows = gathered.shape[1] // lax.axis_size("row")
    columns = lax.slice_in_dim(gathered, 0, lax.axis_size("row") * own_rows, axis=1)
    return lax.psum_scatter(
        lax.dot_general(
            columns, local_grad, (((0,), (0,)), ((), ())), preferred_element_type=jnp.float32
        ),
        "row",
        scatter_dimension=0,
        tiled=True,
    )


def rows_gathered(block, axis):
    pieces = lax.all_gather(block, "row", axis=0, tiled=False)
    pieces = jnp.moveaxis(pieces, 0, axis)
    shape = list(block.shape)
    shape[axis] = shape[axis] * pieces.shape[axis]
    return pieces.reshape(shape)


def rows_gathered_many(blocks_and_axes):
    flat = jnp.concatenate([block.reshape(-1) for block, _ in blocks_and_axes])
    pieces = lax.all_gather(flat, "row", axis=0, tiled=False)
    wholes = []
    offset = 0
    for block, axis in blocks_and_axes:
        piece = pieces[:, offset : offset + block.size].reshape((-1,) + block.shape)
        offset += block.size
        piece = jnp.moveaxis(piece, 0, axis)
        shape = list(block.shape)
        shape[axis] = shape[axis] * piece.shape[axis]
        wholes.append(piece.reshape(shape))
    return wholes


def heads_major(rows, head_size):
    return rows.reshape(rows.shape[0], -1, head_size).transpose(1, 0, 2)


def heads_beside(stacked):
    return stacked.transpose(1, 0, 2).reshape(stacked.shape[1], -1)


def full_norm(row_values, gain_full, shift_full):
    mean_row = jnp.sum(row_values, axis=1, keepdims=True) / D
    var_row = jnp.sum(row_values * row_values, axis=1, keepdims=True) / D - mean_row * mean_row
    inverse = lax.rsqrt(var_row + NORM_EPS)
    normed = (row_values - mean_row) * inverse
    return (normed * gain_full + shift_full, normed, inverse)


def body(
    inputs,
    segments,
    query_weight,
    key_weight,
    value_weight,
    query_bias,
    value_bias,
    output_weight,
    output_bias,
    attn_gain,
    attn_shift,
    up_weight,
    up_bias,
    down_weight,
    down_bias,
    final_gain,
    final_shift,
    cotangent,
):
    head_size = D // HEADS
    score_scale = head_size ** (-0.5)
    labels = segments[0]
    token_rows = inputs.T
    out_grad = cotangent.T.astype(jnp.float32)
    token_count = token_rows.shape[0]
    own_features = token_rows.shape[1]
    own_start = lax.axis_index("col") * own_features
    inputs_full = feature_whole(token_rows)
    qkv_stack = jnp.stack([query_weight, key_weight, value_weight])
    with jax.named_scope("weights_in"):
        qkv_complete, output_rows = rows_gathered_many(((qkv_stack, 1), (output_weight, 1)))
    with jax.named_scope("weights_out"):
        output_complete = lax.all_gather(output_rows, "col", axis=0, tiled=True)
    with jax.named_scope("weights_ffn"):
        up_complete, down_complete = rows_gathered_many(((up_weight, 0), (down_weight, 1)))
    projected = jnp.einsum(
        "td,kdc->ktc", inputs_full, qkv_complete, preferred_element_type=jnp.float32
    )
    queries = heads_major((projected[0] + query_bias).astype(jnp.bfloat16), head_size)
    key_all = heads_major(projected[1].astype(jnp.bfloat16), head_size)
    value_all = heads_major((projected[2] + value_bias).astype(jnp.bfloat16), head_size)
    attended_h, row_max, row_total = attention_forward(
        queries, key_all, value_all, labels, score_scale
    )
    attended = heads_beside(attended_h)
    attended_full = feature_whole(attended)
    output_bias_full = lax.all_gather(output_bias, "col", axis=0, tiled=True)
    gain_one_full = lax.all_gather(attn_gain, "col", axis=0, tiled=True)
    shift_one_full = lax.all_gather(attn_shift, "col", axis=0, tiled=True)
    first_sum_full = (
        inputs_full.astype(jnp.float32)
        + jnp.dot(attended_full, output_complete, preferred_element_type=jnp.float32)
        + output_bias_full
    )
    hidden_full_f, normed_one_full, inverse_one = full_norm(
        first_sum_full, gain_one_full, shift_one_full
    )
    hidden = lax.dynamic_slice_in_dim(hidden_full_f, own_start, own_features, axis=1)
    normed_one = lax.dynamic_slice_in_dim(normed_one_full, own_start, own_features, axis=1)
    hidden_full = hidden_full_f.astype(jnp.bfloat16)
    upped = jnp.dot(hidden_full, up_complete, preferred_element_type=jnp.float32) + up_bias
    acted_f, gelu_pull = jax.vjp(partial(jax.nn.gelu, approximate=False), upped)
    acted = acted_f.astype(jnp.bfloat16)
    ffn_partial = jnp.dot(acted, down_complete, preferred_element_type=jnp.float32)
    second_sum = hidden + feature_sum(ffn_partial) + down_bias
    result, normed_two, inverse_two = norm_forward(second_sum, final_gain, final_shift)
    second_grad, final_gain_grad, final_shift_grad = norm_backward(
        out_grad, normed_two, inverse_two, final_gain
    )
    branch_grad = second_grad.astype(jnp.bfloat16)
    branch_full = feature_whole(branch_grad)
    down_weight_grad = weight_grad(branch_full, acted).T
    acted_grad = lax.dot_general(
        branch_full, down_complete, (((1,), (1,)), ((), ())), preferred_element_type=jnp.float32
    )
    upped_grad = gelu_pull(acted_grad)[0].astype(jnp.bfloat16)
    up_weight_grad = weight_grad(hidden_full, upped_grad)
    hidden_grad = second_grad + feature_sum(
        lax.dot_general(
            upped_grad, up_complete, (((1,), (1,)), ((), ())), preferred_element_type=jnp.float32
        )
    )
    first_grad, attn_gain_grad, attn_shift_grad = norm_backward(
        hidden_grad, normed_one, inverse_one, attn_gain
    )
    attn_branch_grad = first_grad.astype(jnp.bfloat16)
    attn_branch_full = feature_whole(attn_branch_grad)
    output_weight_grad = weight_grad(attn_branch_full, attended).T
    attended_grad = lax.dot_general(
        attn_branch_full, output_rows, (((1,), (1,)), ((), ())), preferred_element_type=jnp.float32
    ).astype(jnp.bfloat16)
    query_grad_h, key_grad_h, value_grad_h = attention_backward(
        queries,
        key_all,
        value_all,
        heads_major(attended_grad, head_size),
        labels,
        row_max,
        row_total,
        score_scale,
    )
    query_grad = heads_beside(query_grad_h)
    key_grad = heads_beside(key_grad_h).astype(jnp.bfloat16)
    value_grad = heads_beside(value_grad_h).astype(jnp.bfloat16)
    column_count = query_weight.shape[1]
    qkv_grads = weight_grad(
        inputs_full, jnp.concatenate([query_grad, key_grad, value_grad], axis=1)
    )
    input_grad = first_grad + feature_sum(
        jnp.einsum(
            "ktc,kdc->td",
            jnp.stack([query_grad, key_grad, value_grad]),
            qkv_complete,
            preferred_element_type=jnp.float32,
        )
    )
    param_totals = lax.psum(
        (
            jnp.sum(query_grad.astype(jnp.float32), axis=0),
            jnp.sum(value_grad.astype(jnp.float32), axis=0),
            jnp.sum(attn_branch_grad.astype(jnp.float32), axis=0),
            attn_gain_grad,
            attn_shift_grad,
            jnp.sum(upped_grad.astype(jnp.float32), axis=0),
            jnp.sum(branch_grad.astype(jnp.float32), axis=0),
            final_gain_grad,
            final_shift_grad,
        ),
        "row",
    )
    return (
        result.astype(jnp.bfloat16).T,
        input_grad.astype(jnp.bfloat16).T,
        qkv_grads[:, :column_count],
        qkv_grads[:, column_count : 2 * column_count],
        qkv_grads[:, 2 * column_count :],
        param_totals[0],
        param_totals[1],
        output_weight_grad,
        param_totals[2],
        param_totals[3],
        param_totals[4],
        up_weight_grad,
        param_totals[5],
        down_weight_grad,
        param_totals[6],
        param_totals[7],
        param_totals[8],
    )


def solution(mesh):
    placed = (
        P("col", "row"),
        P("row", None),
        P("row", "col"),
        P("row", "col"),
        P("row", "col"),
        P("col"),
        P("col"),
        P("col", "row"),
        P("col"),
        P("col"),
        P("col"),
        P("row", "col"),
        P("col"),
        P("col", "row"),
        P("col"),
        P("col"),
        P("col"),
        P("col", "row"),
    )
    return jax.shard_map(
        body,
        mesh=mesh,
        in_specs=placed,
        out_specs=(
            P("col", "row"),
            P("col", "row"),
            P("row", "col"),
            P("row", "col"),
            P("row", "col"),
            P("col"),
            P("col"),
            P("col", "row"),
            P("col"),
            P("col"),
            P("col"),
            P("row", "col"),
            P("col"),
            P("col", "row"),
            P("col"),
            P("col"),
            P("col"),
        ),
        check_vma=False,
    )
```

```python
from functools import partial
import functools

import jax
import jax.numpy as jnp
from jax import lax
from jax.experimental import pallas as pl
from jax.experimental.pallas import tpu as pltpu
from jax.sharding import PartitionSpec as P

D = 768
HEADS = 12
BQ = 256


def _mask(lab_q, lab_k, q0, bq, nk):
    rows = q0 + lax.broadcasted_iota(jnp.int32, (bq, nk), 0)
    cols = lax.broadcasted_iota(jnp.int32, (bq, nk), 1)
    return ((lab_q == lab_k) & (lab_k > 0)) | (rows == cols)


def _fwd_kernel(scale, q_ref, k_ref, v_ref, lq_ref, lk_ref, o_ref, m_ref, l_ref):
    i = pl.program_id(1)
    bq = q_ref.shape[0]
    nk = k_ref.shape[0]
    s = lax.dot_general(q_ref[...], k_ref[...], (((1,), (1,)), ((), ())),
                        preferred_element_type=jnp.float32) * scale
    allowed = _mask(lq_ref[...], lk_ref[...], i * bq, bq, nk)
    s = jnp.where(allowed, s, -1000000000.0)
    m = jnp.max(s, axis=1, keepdims=True)
    e = jnp.exp(s - m)
    l = jnp.sum(e, axis=1, keepdims=True)
    p = (e / l).astype(jnp.bfloat16)
    o_ref[...] = jnp.dot(p, v_ref[...], preferred_element_type=jnp.float32).astype(o_ref.dtype)
    m_ref[...] = m
    l_ref[...] = l


def _bwd_kernel(scale, q_ref, k_ref, v_ref, do_ref, lq_ref, lk_ref, m_ref, l_ref,
                dq_ref, dk_ref, dv_ref):
    i = pl.program_id(1)
    bq = q_ref.shape[0]
    nk = k_ref.shape[0]

    @pl.when(i == 0)
    def _():
        dk_ref[...] = jnp.zeros_like(dk_ref)
        dv_ref[...] = jnp.zeros_like(dv_ref)

    q = q_ref[...]
    k = k_ref[...]
    s = lax.dot_general(q, k, (((1,), (1,)), ((), ())),
                        preferred_element_type=jnp.float32) * scale
    allowed = _mask(lq_ref[...], lk_ref[...], i * bq, bq, nk)
    s = jnp.where(allowed, s, -1000000000.0)
    p = jnp.where(allowed, jnp.exp(s - m_ref[...]) / l_ref[...], 0.0)
    do = do_ref[...]
    dp = lax.dot_general(do, v_ref[...], (((1,), (1,)), ((), ())),
                         preferred_element_type=jnp.float32)
    inner = jnp.sum(p * dp, axis=1, keepdims=True)
    ds = (p * (dp - inner)).astype(jnp.bfloat16)
    dq_ref[...] = (jnp.dot(ds, k, preferred_element_type=jnp.float32) * scale).astype(dq_ref.dtype)
    dk_ref[...] += lax.dot_general(ds, q, (((0,), (0,)), ((), ())),
                                   preferred_element_type=jnp.float32) * scale
    dv_ref[...] += lax.dot_general(p.astype(jnp.bfloat16), do, (((0,), (0,)), ((), ())),
                                   preferred_element_type=jnp.float32)


def attention_forward(q, k, v, labels, scale):
    nh, seq, hd = q.shape
    bq = min(BQ, seq)
    lq = labels.reshape(seq, 1)
    lk = labels.reshape(1, seq)
    grid = (nh, seq // bq)
    qspec = pl.BlockSpec((None, bq, hd), lambda h, i: (h, i, 0))
    kspec = pl.BlockSpec((None, seq, hd), lambda h, i: (h, 0, 0))
    rowspec = pl.BlockSpec((None, bq, 1), lambda h, i: (h, i, 0))
    flops = 4 * nh * seq * seq * hd
    return pl.pallas_call(
        functools.partial(_fwd_kernel, scale),
        grid=grid,
        in_specs=[qspec, kspec, kspec,
                  pl.BlockSpec((bq, 1), lambda h, i: (i, 0)),
                  pl.BlockSpec((1, seq), lambda h, i: (0, 0))],
        out_specs=[qspec, rowspec, rowspec],
        out_shape=[jax.ShapeDtypeStruct((nh, seq, hd), jnp.bfloat16),
                   jax.ShapeDtypeStruct((nh, seq, 1), jnp.float32),
                   jax.ShapeDtypeStruct((nh, seq, 1), jnp.float32)],
        compiler_params=pltpu.CompilerParams(
            dimension_semantics=("parallel", "arbitrary"),
            vmem_limit_bytes=48 * 1024 * 1024),
        cost_estimate=pl.CostEstimate(flops=flops, transcendentals=nh * seq * seq,
                                      bytes_accessed=4 * nh * seq * hd * 2),
    )(q, k, v, lq, lk)


def attention_backward(q, k, v, do, labels, m, l, scale):
    nh, seq, hd = q.shape
    bq = min(BQ, seq)
    lq = labels.reshape(seq, 1)
    lk = labels.reshape(1, seq)
    grid = (nh, seq // bq)
    qspec = pl.BlockSpec((None, bq, hd), lambda h, i: (h, i, 0))
    kspec = pl.BlockSpec((None, seq, hd), lambda h, i: (h, 0, 0))
    rowspec = pl.BlockSpec((None, bq, 1), lambda h, i: (h, i, 0))
    flops = 10 * nh * seq * seq * hd
    return pl.pallas_call(
        functools.partial(_bwd_kernel, scale),
        grid=grid,
        in_specs=[qspec, kspec, kspec, qspec,
                  pl.BlockSpec((bq, 1), lambda h, i: (i, 0)),
                  pl.BlockSpec((1, seq), lambda h, i: (0, 0)),
                  rowspec, rowspec],
        out_specs=[qspec, kspec, kspec],
        out_shape=[jax.ShapeDtypeStruct((nh, seq, hd), jnp.bfloat16),
                   jax.ShapeDtypeStruct((nh, seq, hd), jnp.float32),
                   jax.ShapeDtypeStruct((nh, seq, hd), jnp.float32)],
        compiler_params=pltpu.CompilerParams(
            dimension_semantics=("parallel", "arbitrary"),
            vmem_limit_bytes=48 * 1024 * 1024),
        cost_estimate=pl.CostEstimate(flops=flops, transcendentals=nh * seq * seq,
                                      bytes_accessed=8 * nh * seq * hd * 2),
    )(q, k, v, do, lq, lk, m, l)


NORM_EPS = 1e-06


def feature_whole(blocked):
    return lax.all_gather(blocked, "col", axis=1, tiled=True)


def feature_sum(partial_rows):
    return lax.psum_scatter(partial_rows, "col", scatter_dimension=1, tiled=True)


def row_totals(first_term, second_term):
    return lax.psum((jnp.sum(first_term, axis=1), jnp.sum(second_term, axis=1)), "col")


def norm_forward(row_values, gain_row, shift_row):
    totals, squares = row_totals(row_values, row_values * row_values)
    mean_row = (totals / D)[:, None]
    var_row = (squares / D)[:, None] - mean_row * mean_row
    inverse = lax.rsqrt(var_row + NORM_EPS)
    normed = (row_values - mean_row) * inverse
    return (normed * gain_row + shift_row, normed, inverse)


def norm_backward(grad_rows, normed, inverse, gain_row):
    scaled = grad_rows * gain_row
    totals, along = row_totals(scaled, scaled * normed)
    back_rows = inverse * (scaled - (totals / D)[:, None] - normed * (along / D)[:, None])
    return (back_rows, jnp.sum(grad_rows * normed, axis=0), jnp.sum(grad_rows, axis=0))


def project_in(gathered, stacked):
    complete = lax.all_gather(stacked, "row", axis=1, tiled=True)
    return (
        jnp.einsum("td,kdc->ktc", gathered, complete, preferred_element_type=jnp.float32),
        complete,
    )


def project_in_back(grad_stack, stacked, complete):
    complete = lax.all_gather(stacked, "row", axis=1, tiled=True)
    return jnp.einsum("ktc,kdc->td", grad_stack, complete, preferred_element_type=jnp.float32)


def columns_whole(weight_block):
    return lax.all_gather(weight_block, "row", axis=1, tiled=True)


def project_out_back(grad_full, weight_block, complete):
    contract = (((1,), (1,)), ((), ()))
    complete = lax.all_gather(weight_block, "row", axis=1, tiled=True)
    return lax.dot_general(grad_full, complete, contract, preferred_element_type=jnp.float32)


def row_scatter_sum(partial_rows):
    count = lax.axis_size("row")
    me = lax.axis_index("row")
    blocks = partial_rows.reshape((count, partial_rows.shape[0] // count) + partial_rows.shape[1:])
    total = blocks[me]
    for shift in range(1, count):
        outgoing = blocks[lax.rem(me + shift, count)]
        total = total + lax.ppermute(
            outgoing, "row", [(i, (i + shift) % count) for i in range(count)]
        )
    return total


def row_sum(values):
    count = lax.axis_size("row")
    total = values
    for shift in range(1, count):
        total = total + lax.ppermute(
            values, "row", [(i, (i + shift) % count) for i in range(count)]
        )
    return total


def weight_grad(gathered, local_grad):
    return row_scatter_sum(
        lax.dot_general(
            gathered, local_grad, (((0,), (0,)), ((), ())), preferred_element_type=jnp.float32
        )
    )


def rows_gathered_many(blocks_and_axes):
    flat = jnp.concatenate([block.reshape(-1) for block, _ in blocks_and_axes])
    pieces = lax.all_gather(flat, "row", axis=0, tiled=False)
    wholes = []
    offset = 0
    for block, axis in blocks_and_axes:
        piece = pieces[:, offset : offset + block.size].reshape((-1,) + block.shape)
        offset += block.size
        piece = jnp.moveaxis(piece, 0, axis)
        shape = list(block.shape)
        shape[axis] = shape[axis] * piece.shape[axis]
        wholes.append(piece.reshape(shape))
    return wholes


def heads_major(rows, head_size):
    return rows.reshape(rows.shape[0], -1, head_size).transpose(1, 0, 2)


def heads_beside(stacked):
    return stacked.transpose(1, 0, 2).reshape(stacked.shape[1], -1)


def full_norm(row_values, gain_full, shift_full):
    mean_row = jnp.sum(row_values, axis=1, keepdims=True) / D
    var_row = jnp.sum(row_values * row_values, axis=1, keepdims=True) / D - mean_row * mean_row
    inverse = lax.rsqrt(var_row + NORM_EPS)
    normed = (row_values - mean_row) * inverse
    return (normed * gain_full + shift_full, normed, inverse)


def body(
    inputs,
    segments,
    query_weight,
    key_weight,
    value_weight,
    query_bias,
    value_bias,
    output_weight,
    output_bias,
    attn_gain,
    attn_shift,
    up_weight,
    up_bias,
    down_weight,
    down_bias,
    final_gain,
    final_shift,
    cotangent,
):
    head_size = D // HEADS
    score_scale = head_size ** (-0.5)
    labels = segments[0]
    token_rows = inputs.T
    out_grad = cotangent.T.astype(jnp.float32)
    token_count = token_rows.shape[0]
    own_features = token_rows.shape[1]
    own_start = lax.axis_index("col") * own_features
    inputs_full = feature_whole(token_rows)
    qkv_stack = jnp.stack([query_weight, key_weight, value_weight])
    with jax.named_scope("weights_in"):
        qkv_complete, output_rows = rows_gathered_many(((qkv_stack, 1), (output_weight, 1)))
    with jax.named_scope("weights_out"):
        output_complete = lax.all_gather(output_rows, "col", axis=0, tiled=True)
    with jax.named_scope("weights_ffn"):
        up_complete, down_complete = rows_gathered_many(((up_weight, 0), (down_weight, 1)))
    projected = jnp.einsum(
        "td,kdc->ktc", inputs_full, qkv_complete, preferred_element_type=jnp.float32
    )
    queries = heads_major((projected[0] + query_bias).astype(jnp.bfloat16), head_size)
    key_all = heads_major(projected[1].astype(jnp.bfloat16), head_size)
    value_all = heads_major((projected[2] + value_bias).astype(jnp.bfloat16), head_size)
    attended_h, row_max, row_total = attention_forward(
        queries, key_all, value_all, labels, score_scale
    )
    attended = heads_beside(attended_h)
    attended_full = feature_whole(attended)
    output_bias_full = lax.all_gather(output_bias, "col", axis=0, tiled=True)
    gain_one_full = lax.all_gather(attn_gain, "col", axis=0, tiled=True)
    shift_one_full = lax.all_gather(attn_shift, "col", axis=0, tiled=True)
    first_sum_full = (
        inputs_full.astype(jnp.float32)
        + jnp.dot(attended_full, output_complete, preferred_element_type=jnp.float32)
        + output_bias_full
    )
    hidden_full_f, normed_one_full, inverse_one = full_norm(
        first_sum_full, gain_one_full, shift_one_full
    )
    hidden = lax.dynamic_slice_in_dim(hidden_full_f, own_start, own_features, axis=1)
    normed_one = lax.dynamic_slice_in_dim(normed_one_full, own_start, own_features, axis=1)
    hidden_full = hidden_full_f.astype(jnp.bfloat16)
    upped = jnp.dot(hidden_full, up_complete, preferred_element_type=jnp.float32) + up_bias
    acted_f, gelu_pull = jax.vjp(partial(jax.nn.gelu, approximate=False), upped)
    acted = acted_f.astype(jnp.bfloat16)
    ffn_partial = jnp.dot(acted, down_complete, preferred_element_type=jnp.float32)
    second_sum = hidden + feature_sum(ffn_partial) + down_bias
    result, normed_two, inverse_two = norm_forward(second_sum, final_gain, final_shift)
    second_grad, final_gain_grad, final_shift_grad = norm_backward(
        out_grad, normed_two, inverse_two, final_gain
    )
    branch_grad = second_grad.astype(jnp.bfloat16)
    branch_full = feature_whole(branch_grad)
    down_weight_grad = weight_grad(branch_full, acted).T
    acted_grad = lax.dot_general(
        branch_full, down_complete, (((1,), (1,)), ((), ())), preferred_element_type=jnp.float32
    )
    upped_grad = gelu_pull(acted_grad)[0].astype(jnp.bfloat16)
    up_weight_grad = weight_grad(hidden_full, upped_grad)
    hidden_grad = second_grad + feature_sum(
        lax.dot_general(
            upped_grad, up_complete, (((1,), (1,)), ((), ())), preferred_element_type=jnp.float32
        )
    )
    first_grad, attn_gain_grad, attn_shift_grad = norm_backward(
        hidden_grad, normed_one, inverse_one, attn_gain
    )
    attn_branch_grad = first_grad.astype(jnp.bfloat16)
    attn_branch_full = feature_whole(attn_branch_grad)
    output_weight_grad = weight_grad(attn_branch_full, attended).T
    attended_grad = lax.dot_general(
        attn_branch_full, output_rows, (((1,), (1,)), ((), ())), preferred_element_type=jnp.float32
    ).astype(jnp.bfloat16)
    query_grad_h, key_grad_h, value_grad_h = attention_backward(
        queries,
        key_all,
        value_all,
        heads_major(attended_grad, head_size),
        labels,
        row_max,
        row_total,
        score_scale,
    )
    query_grad = heads_beside(query_grad_h)
    key_grad = heads_beside(key_grad_h).astype(jnp.bfloat16)
    value_grad = heads_beside(value_grad_h).astype(jnp.bfloat16)
    column_count = query_weight.shape[1]
    qkv_grads = weight_grad(
        inputs_full, jnp.concatenate([query_grad, key_grad, value_grad], axis=1)
    )
    input_grad = first_grad + feature_sum(
        jnp.einsum(
            "ktc,kdc->td",
            jnp.stack([query_grad, key_grad, value_grad]),
            qkv_complete,
            preferred_element_type=jnp.float32,
        )
    )
    param_parts = (
        jnp.sum(query_grad.astype(jnp.float32), axis=0),
        jnp.sum(value_grad.astype(jnp.float32), axis=0),
        jnp.sum(attn_branch_grad.astype(jnp.float32), axis=0),
        attn_gain_grad,
        attn_shift_grad,
        jnp.sum(upped_grad.astype(jnp.float32), axis=0),
        jnp.sum(branch_grad.astype(jnp.float32), axis=0),
        final_gain_grad,
        final_shift_grad,
    )
    param_flat = row_sum(jnp.concatenate(param_parts))
    param_totals = []
    offset = 0
    for part in param_parts:
        param_totals.append(param_flat[offset : offset + part.shape[0]])
        offset += part.shape[0]
    return (
        result.astype(jnp.bfloat16).T,
        input_grad.astype(jnp.bfloat16).T,
        qkv_grads[:, :column_count],
        qkv_grads[:, column_count : 2 * column_count],
        qkv_grads[:, 2 * column_count :],
        param_totals[0],
        param_totals[1],
        output_weight_grad,
        param_totals[2],
        param_totals[3],
        param_totals[4],
        up_weight_grad,
        param_totals[5],
        down_weight_grad,
        param_totals[6],
        param_totals[7],
        param_totals[8],
    )


def solution(mesh):
    placed = (
        P("col", "row"),
        P("row", None),
        P("row", "col"),
        P("row", "col"),
        P("row", "col"),
        P("col"),
        P("col"),
        P("col", "row"),
        P("col"),
        P("col"),
        P("col"),
        P("row", "col"),
        P("col"),
        P("col", "row"),
        P("col"),
        P("col"),
        P("col"),
        P("col", "row"),
    )
    return jax.shard_map(
        body,
        mesh=mesh,
        in_specs=placed,
        out_specs=(
            P("col", "row"),
            P("col", "row"),
            P("row", "col"),
            P("row", "col"),
            P("row", "col"),
            P("col"),
            P("col"),
            P("col", "row"),
            P("col"),
            P("col"),
            P("col"),
            P("row", "col"),
            P("col"),
            P("col", "row"),
            P("col"),
            P("col"),
            P("col"),
        ),
        check_vma=False,
    )
```

```python
from functools import partial
import functools

import jax
import jax.numpy as jnp
from jax import lax
from jax.experimental import pallas as pl
from jax.experimental.pallas import tpu as pltpu
from jax.sharding import PartitionSpec as P

D = 768
HEADS = 12
BQ = 256


def _mask(lab_q, lab_k, q0, bq, nk):
    rows = q0 + lax.broadcasted_iota(jnp.int32, (bq, nk), 0)
    cols = lax.broadcasted_iota(jnp.int32, (bq, nk), 1)
    return ((lab_q == lab_k) & (lab_k > 0)) | (rows == cols)


def _fwd_kernel(scale, q_ref, k_ref, v_ref, lq_ref, lk_ref, o_ref, m_ref, l_ref):
    i = pl.program_id(1)
    bq = q_ref.shape[0]
    nk = k_ref.shape[0]
    s = lax.dot_general(q_ref[...], k_ref[...], (((1,), (1,)), ((), ())),
                        preferred_element_type=jnp.float32) * scale
    allowed = _mask(lq_ref[...], lk_ref[...], i * bq, bq, nk)
    s = jnp.where(allowed, s, -1000000000.0)
    m = jnp.max(s, axis=1, keepdims=True)
    e = jnp.exp(s - m)
    l = jnp.sum(e, axis=1, keepdims=True)
    p = (e / l).astype(jnp.bfloat16)
    o_ref[...] = jnp.dot(p, v_ref[...], preferred_element_type=jnp.float32).astype(o_ref.dtype)
    m_ref[...] = m
    l_ref[...] = l


def _bwd_kernel(scale, q_ref, k_ref, v_ref, do_ref, lq_ref, lk_ref, m_ref, l_ref,
                dq_ref, dk_ref, dv_ref):
    i = pl.program_id(1)
    bq = q_ref.shape[0]
    nk = k_ref.shape[0]

    @pl.when(i == 0)
    def _():
        dk_ref[...] = jnp.zeros_like(dk_ref)
        dv_ref[...] = jnp.zeros_like(dv_ref)

    q = q_ref[...]
    k = k_ref[...]
    s = lax.dot_general(q, k, (((1,), (1,)), ((), ())),
                        preferred_element_type=jnp.float32) * scale
    allowed = _mask(lq_ref[...], lk_ref[...], i * bq, bq, nk)
    s = jnp.where(allowed, s, -1000000000.0)
    p = jnp.where(allowed, jnp.exp(s - m_ref[...]) / l_ref[...], 0.0)
    do = do_ref[...]
    dp = lax.dot_general(do, v_ref[...], (((1,), (1,)), ((), ())),
                         preferred_element_type=jnp.float32)
    inner = jnp.sum(p * dp, axis=1, keepdims=True)
    ds = (p * (dp - inner)).astype(jnp.bfloat16)
    dq_ref[...] = (jnp.dot(ds, k, preferred_element_type=jnp.float32) * scale).astype(dq_ref.dtype)
    dk_ref[...] += lax.dot_general(ds, q, (((0,), (0,)), ((), ())),
                                   preferred_element_type=jnp.float32) * scale
    dv_ref[...] += lax.dot_general(p.astype(jnp.bfloat16), do, (((0,), (0,)), ((), ())),
                                   preferred_element_type=jnp.float32)


def attention_forward(q, k, v, labels, scale):
    nh, seq, hd = q.shape
    bq = min(BQ, seq)
    lq = labels.reshape(seq, 1)
    lk = labels.reshape(1, seq)
    grid = (nh, seq // bq)
    qspec = pl.BlockSpec((None, bq, hd), lambda h, i: (h, i, 0))
    kspec = pl.BlockSpec((None, seq, hd), lambda h, i: (h, 0, 0))
    rowspec = pl.BlockSpec((None, bq, 1), lambda h, i: (h, i, 0))
    flops = 4 * nh * seq * seq * hd
    return pl.pallas_call(
        functools.partial(_fwd_kernel, scale),
        grid=grid,
        in_specs=[qspec, kspec, kspec,
                  pl.BlockSpec((bq, 1), lambda h, i: (i, 0)),
                  pl.BlockSpec((1, seq), lambda h, i: (0, 0))],
        out_specs=[qspec, rowspec, rowspec],
        out_shape=[jax.ShapeDtypeStruct((nh, seq, hd), jnp.bfloat16),
                   jax.ShapeDtypeStruct((nh, seq, 1), jnp.float32),
                   jax.ShapeDtypeStruct((nh, seq, 1), jnp.float32)],
        compiler_params=pltpu.CompilerParams(
            dimension_semantics=("parallel", "arbitrary"),
            vmem_limit_bytes=48 * 1024 * 1024),
        cost_estimate=pl.CostEstimate(flops=flops, transcendentals=nh * seq * seq,
                                      bytes_accessed=4 * nh * seq * hd * 2),
    )(q, k, v, lq, lk)


def attention_backward(q, k, v, do, labels, m, l, scale):
    nh, seq, hd = q.shape
    bq = min(BQ, seq)
    lq = labels.reshape(seq, 1)
    lk = labels.reshape(1, seq)
    grid = (nh, seq // bq)
    qspec = pl.BlockSpec((None, bq, hd), lambda h, i: (h, i, 0))
    kspec = pl.BlockSpec((None, seq, hd), lambda h, i: (h, 0, 0))
    rowspec = pl.BlockSpec((None, bq, 1), lambda h, i: (h, i, 0))
    flops = 10 * nh * seq * seq * hd
    return pl.pallas_call(
        functools.partial(_bwd_kernel, scale),
        grid=grid,
        in_specs=[qspec, kspec, kspec, qspec,
                  pl.BlockSpec((bq, 1), lambda h, i: (i, 0)),
                  pl.BlockSpec((1, seq), lambda h, i: (0, 0)),
                  rowspec, rowspec],
        out_specs=[qspec, kspec, kspec],
        out_shape=[jax.ShapeDtypeStruct((nh, seq, hd), jnp.bfloat16),
                   jax.ShapeDtypeStruct((nh, seq, hd), jnp.float32),
                   jax.ShapeDtypeStruct((nh, seq, hd), jnp.float32)],
        compiler_params=pltpu.CompilerParams(
            dimension_semantics=("parallel", "arbitrary"),
            vmem_limit_bytes=48 * 1024 * 1024),
        cost_estimate=pl.CostEstimate(flops=flops, transcendentals=nh * seq * seq,
                                      bytes_accessed=8 * nh * seq * hd * 2),
    )(q, k, v, do, lq, lk, m, l)


NORM_EPS = 1e-06


def feature_whole(blocked):
    return lax.all_gather(blocked, "col", axis=1, tiled=True)


def feature_sum(partial_rows):
    return lax.psum_scatter(partial_rows, "col", scatter_dimension=1, tiled=True)


def row_totals(first_term, second_term):
    return lax.psum((jnp.sum(first_term, axis=1), jnp.sum(second_term, axis=1)), "col")


def norm_forward(row_values, gain_row, shift_row):
    totals, squares = row_totals(row_values, row_values * row_values)
    mean_row = (totals / D)[:, None]
    var_row = (squares / D)[:, None] - mean_row * mean_row
    inverse = lax.rsqrt(var_row + NORM_EPS)
    normed = (row_values - mean_row) * inverse
    return (normed * gain_row + shift_row, normed, inverse)


def norm_backward(grad_rows, normed, inverse, gain_row):
    scaled = grad_rows * gain_row
    totals, along = row_totals(scaled, scaled * normed)
    back_rows = inverse * (scaled - (totals / D)[:, None] - normed * (along / D)[:, None])
    return (back_rows, jnp.sum(grad_rows * normed, axis=0), jnp.sum(grad_rows, axis=0))


def project_in(gathered, stacked):
    complete = lax.all_gather(stacked, "row", axis=1, tiled=True)
    return (
        jnp.einsum("td,kdc->ktc", gathered, complete, preferred_element_type=jnp.float32),
        complete,
    )


def project_in_back(grad_stack, stacked, complete):
    complete = lax.all_gather(stacked, "row", axis=1, tiled=True)
    return jnp.einsum("ktc,kdc->td", grad_stack, complete, preferred_element_type=jnp.float32)


def columns_whole(weight_block):
    return lax.all_gather(weight_block, "row", axis=1, tiled=True)


def project_out_back(grad_full, weight_block, complete):
    contract = (((1,), (1,)), ((), ()))
    complete = lax.all_gather(weight_block, "row", axis=1, tiled=True)
    return lax.dot_general(grad_full, complete, contract, preferred_element_type=jnp.float32)


def row_scatter_sum(blocks):
    count = lax.axis_size("row")
    me = lax.axis_index("row")
    total = blocks[me]
    for shift in range(1, count):
        outgoing = blocks[lax.rem(me + shift, count)]
        total = total + lax.ppermute(
            outgoing, "row", [(i, (i + shift) % count) for i in range(count)]
        )
    return total


def row_sum(values):
    count = lax.axis_size("row")
    total = values
    for shift in range(1, count):
        total = total + lax.ppermute(
            values, "row", [(i, (i + shift) % count) for i in range(count)]
        )
    return total


def row_gather(values, axis="row"):
    count = lax.axis_size(axis)
    me = lax.axis_index(axis)
    arrived = [values]
    for shift in range(1, count):
        arrived.append(
            lax.ppermute(values, axis, [(i, (i + shift) % count) for i in range(count)])
        )
    stacked = jnp.stack(arrived)
    order = lax.rem(me - jnp.arange(count) + count, count)
    return stacked[order]


def weight_partial(gathered, local_grad):
    return lax.dot_general(
        gathered, local_grad, (((0,), (0,)), ((), ())), preferred_element_type=jnp.float32
    )


def weight_grad(gathered, local_grad):
    return row_scatter_sum(
        lax.dot_general(
            gathered, local_grad, (((0,), (0,)), ((), ())), preferred_element_type=jnp.float32
        )
    )


def rows_gathered_many(blocks_and_axes):
    flat = jnp.concatenate([block.reshape(-1) for block, _ in blocks_and_axes])
    pieces = row_gather(flat)
    wholes = []
    offset = 0
    for block, axis in blocks_and_axes:
        piece = pieces[:, offset : offset + block.size].reshape((-1,) + block.shape)
        offset += block.size
        piece = jnp.moveaxis(piece, 0, axis)
        shape = list(block.shape)
        shape[axis] = shape[axis] * piece.shape[axis]
        wholes.append(piece.reshape(shape))
    return wholes


def heads_major(rows, head_size):
    return rows.reshape(rows.shape[0], -1, head_size).transpose(1, 0, 2)


def heads_beside(stacked):
    return stacked.transpose(1, 0, 2).reshape(stacked.shape[1], -1)


def full_norm(row_values, gain_full, shift_full):
    mean_row = jnp.sum(row_values, axis=1, keepdims=True) / D
    var_row = jnp.sum(row_values * row_values, axis=1, keepdims=True) / D - mean_row * mean_row
    inverse = lax.rsqrt(var_row + NORM_EPS)
    normed = (row_values - mean_row) * inverse
    return (normed * gain_full + shift_full, normed, inverse)


def body(
    inputs,
    segments,
    query_weight,
    key_weight,
    value_weight,
    query_bias,
    value_bias,
    output_weight,
    output_bias,
    attn_gain,
    attn_shift,
    up_weight,
    up_bias,
    down_weight,
    down_bias,
    final_gain,
    final_shift,
    cotangent,
):
    head_size = D // HEADS
    score_scale = head_size ** (-0.5)
    labels = segments[0]
    token_rows = inputs.T
    out_grad = cotangent.T.astype(jnp.float32)
    token_count = token_rows.shape[0]
    own_features = token_rows.shape[1]
    own_start = lax.axis_index("col") * own_features
    inputs_full = feature_whole(token_rows)
    qkv_stack = jnp.stack([query_weight, key_weight, value_weight])
    with jax.named_scope("weights_in"):
        qkv_complete, output_rows, up_complete, down_complete = rows_gathered_many(
            ((qkv_stack, 1), (output_weight, 1), (up_weight, 0), (down_weight, 1))
        )
    with jax.named_scope("weights_out"):
        output_complete = lax.all_gather(output_rows, "col", axis=0, tiled=True)
    projected = jnp.einsum(
        "td,kdc->ktc", inputs_full, qkv_complete, preferred_element_type=jnp.float32
    )
    queries = heads_major((projected[0] + query_bias).astype(jnp.bfloat16), head_size)
    key_all = heads_major(projected[1].astype(jnp.bfloat16), head_size)
    value_all = heads_major((projected[2] + value_bias).astype(jnp.bfloat16), head_size)
    attended_h, row_max, row_total = attention_forward(
        queries, key_all, value_all, labels, score_scale
    )
    attended = heads_beside(attended_h)
    attended_full = feature_whole(attended)
    vectors_full = row_gather(jnp.stack([output_bias, attn_gain, attn_shift]), "col")
    output_bias_full, gain_one_full, shift_one_full = (
        vectors_full[:, which].reshape(-1) for which in range(3)
    )
    first_sum_full = (
        inputs_full.astype(jnp.float32)
        + jnp.dot(attended_full, output_complete, preferred_element_type=jnp.float32)
        + output_bias_full
    )
    hidden_full_f, normed_one_full, inverse_one = full_norm(
        first_sum_full, gain_one_full, shift_one_full
    )
    hidden = lax.dynamic_slice_in_dim(hidden_full_f, own_start, own_features, axis=1)
    normed_one = lax.dynamic_slice_in_dim(normed_one_full, own_start, own_features, axis=1)
    hidden_full = hidden_full_f.astype(jnp.bfloat16)
    upped = jnp.dot(hidden_full, up_complete, preferred_element_type=jnp.float32) + up_bias
    acted_f, gelu_pull = jax.vjp(partial(jax.nn.gelu, approximate=False), upped)
    acted = acted_f.astype(jnp.bfloat16)
    ffn_partial = jnp.dot(acted, down_complete, preferred_element_type=jnp.float32)
    second_sum = hidden + feature_sum(ffn_partial) + down_bias
    result, normed_two, inverse_two = norm_forward(second_sum, final_gain, final_shift)
    second_grad, final_gain_grad, final_shift_grad = norm_backward(
        out_grad, normed_two, inverse_two, final_gain
    )
    branch_grad = second_grad.astype(jnp.bfloat16)
    branch_full = feature_whole(branch_grad)
    down_partial = weight_partial(branch_full, acted)
    acted_grad = lax.dot_general(
        branch_full, down_complete, (((1,), (1,)), ((), ())), preferred_element_type=jnp.float32
    )
    upped_grad = gelu_pull(acted_grad)[0].astype(jnp.bfloat16)
    up_partial = weight_partial(hidden_full, upped_grad)
    hidden_grad = second_grad + feature_sum(
        lax.dot_general(
            upped_grad, up_complete, (((1,), (1,)), ((), ())), preferred_element_type=jnp.float32
        )
    )
    first_grad, attn_gain_grad, attn_shift_grad = norm_backward(
        hidden_grad, normed_one, inverse_one, attn_gain
    )
    attn_branch_grad = first_grad.astype(jnp.bfloat16)
    attn_branch_full = feature_whole(attn_branch_grad)
    output_partial = weight_partial(attn_branch_full, attended)
    attended_grad = lax.dot_general(
        attn_branch_full, output_rows, (((1,), (1,)), ((), ())), preferred_element_type=jnp.float32
    ).astype(jnp.bfloat16)
    query_grad_h, key_grad_h, value_grad_h = attention_backward(
        queries,
        key_all,
        value_all,
        heads_major(attended_grad, head_size),
        labels,
        row_max,
        row_total,
        score_scale,
    )
    query_grad = heads_beside(query_grad_h)
    key_grad = heads_beside(key_grad_h).astype(jnp.bfloat16)
    value_grad = heads_beside(value_grad_h).astype(jnp.bfloat16)
    column_count = query_weight.shape[1]
    qkv_partial = weight_partial(
        inputs_full, jnp.concatenate([query_grad, key_grad, value_grad], axis=1)
    )
    input_grad = first_grad + feature_sum(
        jnp.einsum(
            "ktc,kdc->td",
            jnp.stack([query_grad, key_grad, value_grad]),
            qkv_complete,
            preferred_element_type=jnp.float32,
        )
    )
    param_parts = (
        jnp.sum(query_grad.astype(jnp.float32), axis=0),
        jnp.sum(value_grad.astype(jnp.float32), axis=0),
        jnp.sum(attn_branch_grad.astype(jnp.float32), axis=0),
        attn_gain_grad,
        attn_shift_grad,
        jnp.sum(upped_grad.astype(jnp.float32), axis=0),
        jnp.sum(branch_grad.astype(jnp.float32), axis=0),
        final_gain_grad,
        final_shift_grad,
    )
    param_flat = jnp.concatenate(param_parts)
    row_count = lax.axis_size("row")
    partials = (down_partial, up_partial, output_partial, qkv_partial)
    joined = jnp.concatenate(partials, axis=1)
    joined = joined.reshape(row_count, joined.shape[0] // row_count, joined.shape[1])
    extra = jnp.broadcast_to(param_flat, (row_count, 1, param_flat.shape[0]))
    if param_flat.shape[0] == joined.shape[2]:
        summed = row_scatter_sum(jnp.concatenate([joined, extra], axis=1))
        param_flat = summed[-1]
        summed = summed[:-1]
    else:
        summed = row_scatter_sum(joined)
        param_flat = row_sum(param_flat)
    grads_own = []
    offset = 0
    for part in partials:
        grads_own.append(summed[:, offset : offset + part.shape[1]])
        offset += part.shape[1]
    down_weight_grad = grads_own[0].T
    up_weight_grad = grads_own[1]
    output_weight_grad = grads_own[2].T
    qkv_grads = grads_own[3]
    param_totals = []
    offset = 0
    for part in param_parts:
        param_totals.append(param_flat[offset : offset + part.shape[0]])
        offset += part.shape[0]
    return (
        result.astype(jnp.bfloat16).T,
        input_grad.astype(jnp.bfloat16).T,
        qkv_grads[:, :column_count],
        qkv_grads[:, column_count : 2 * column_count],
        qkv_grads[:, 2 * column_count :],
        param_totals[0],
        param_totals[1],
        output_weight_grad,
        param_totals[2],
        param_totals[3],
        param_totals[4],
        up_weight_grad,
        param_totals[5],
        down_weight_grad,
        param_totals[6],
        param_totals[7],
        param_totals[8],
    )


def solution(mesh):
    placed = (
        P("col", "row"),
        P("row", None),
        P("row", "col"),
        P("row", "col"),
        P("row", "col"),
        P("col"),
        P("col"),
        P("col", "row"),
        P("col"),
        P("col"),
        P("col"),
        P("row", "col"),
        P("col"),
        P("col", "row"),
        P("col"),
        P("col"),
        P("col"),
        P("col", "row"),
    )
    return jax.shard_map(
        body,
        mesh=mesh,
        in_specs=placed,
        out_specs=(
            P("col", "row"),
            P("col", "row"),
            P("row", "col"),
            P("row", "col"),
            P("row", "col"),
            P("col"),
            P("col"),
            P("col", "row"),
            P("col"),
            P("col"),
            P("col"),
            P("row", "col"),
            P("col"),
            P("col", "row"),
            P("col"),
            P("col"),
            P("col"),
        ),
        check_vma=False,
    )
```

```python
from functools import partial
import functools

import jax
import jax.numpy as jnp
from jax import lax
from jax.experimental import pallas as pl
from jax.experimental.pallas import tpu as pltpu
from jax.sharding import PartitionSpec as P

D = 768
HEADS = 12
BQ = 256


def _mask(lab_q, lab_k, q0, bq, nk):
    rows = q0 + lax.broadcasted_iota(jnp.int32, (bq, nk), 0)
    cols = lax.broadcasted_iota(jnp.int32, (bq, nk), 1)
    return ((lab_q == lab_k) & (lab_k > 0)) | (rows == cols)


def _fwd_kernel(scale, q_ref, k_ref, v_ref, lq_ref, lk_ref, o_ref, m_ref, l_ref):
    i = pl.program_id(1)
    bq = q_ref.shape[0]
    nk = k_ref.shape[0]
    s = lax.dot_general(q_ref[...], k_ref[...], (((1,), (1,)), ((), ())),
                        preferred_element_type=jnp.float32) * scale
    allowed = _mask(lq_ref[...], lk_ref[...], i * bq, bq, nk)
    s = jnp.where(allowed, s, -1000000000.0)
    m = jnp.max(s, axis=1, keepdims=True)
    e = jnp.exp(s - m)
    l = jnp.sum(e, axis=1, keepdims=True)
    p = (e / l).astype(jnp.bfloat16)
    o_ref[...] = jnp.dot(p, v_ref[...], preferred_element_type=jnp.float32).astype(o_ref.dtype)
    m_ref[...] = m
    l_ref[...] = l


def _bwd_kernel(scale, q_ref, k_ref, v_ref, do_ref, lq_ref, lk_ref, m_ref, l_ref,
                dq_ref, dk_ref, dv_ref):
    i = pl.program_id(1)
    bq = q_ref.shape[0]
    nk = k_ref.shape[0]

    @pl.when(i == 0)
    def _():
        dk_ref[...] = jnp.zeros_like(dk_ref)
        dv_ref[...] = jnp.zeros_like(dv_ref)

    q = q_ref[...]
    k = k_ref[...]
    s = lax.dot_general(q, k, (((1,), (1,)), ((), ())),
                        preferred_element_type=jnp.float32) * scale
    allowed = _mask(lq_ref[...], lk_ref[...], i * bq, bq, nk)
    s = jnp.where(allowed, s, -1000000000.0)
    p = jnp.where(allowed, jnp.exp(s - m_ref[...]) / l_ref[...], 0.0)
    do = do_ref[...]
    dp = lax.dot_general(do, v_ref[...], (((1,), (1,)), ((), ())),
                         preferred_element_type=jnp.float32)
    inner = jnp.sum(p * dp, axis=1, keepdims=True)
    ds = (p * (dp - inner)).astype(jnp.bfloat16)
    dq_ref[...] = (jnp.dot(ds, k, preferred_element_type=jnp.float32) * scale).astype(dq_ref.dtype)
    dk_ref[...] += lax.dot_general(ds, q, (((0,), (0,)), ((), ())),
                                   preferred_element_type=jnp.float32) * scale
    dv_ref[...] += lax.dot_general(p.astype(jnp.bfloat16), do, (((0,), (0,)), ((), ())),
                                   preferred_element_type=jnp.float32)


def attention_forward(q, k, v, labels, scale):
    nh, seq, hd = q.shape
    bq = min(BQ, seq)
    lq = labels.reshape(seq, 1)
    lk = labels.reshape(1, seq)
    grid = (nh, seq // bq)
    qspec = pl.BlockSpec((None, bq, hd), lambda h, i: (h, i, 0))
    kspec = pl.BlockSpec((None, seq, hd), lambda h, i: (h, 0, 0))
    rowspec = pl.BlockSpec((None, bq, 1), lambda h, i: (h, i, 0))
    flops = 4 * nh * seq * seq * hd
    return pl.pallas_call(
        functools.partial(_fwd_kernel, scale),
        grid=grid,
        in_specs=[qspec, kspec, kspec,
                  pl.BlockSpec((bq, 1), lambda h, i: (i, 0)),
                  pl.BlockSpec((1, seq), lambda h, i: (0, 0))],
        out_specs=[qspec, rowspec, rowspec],
        out_shape=[jax.ShapeDtypeStruct((nh, seq, hd), jnp.bfloat16),
                   jax.ShapeDtypeStruct((nh, seq, 1), jnp.float32),
                   jax.ShapeDtypeStruct((nh, seq, 1), jnp.float32)],
        compiler_params=pltpu.CompilerParams(
            dimension_semantics=("parallel", "arbitrary"),
            vmem_limit_bytes=48 * 1024 * 1024),
        cost_estimate=pl.CostEstimate(flops=flops, transcendentals=nh * seq * seq,
                                      bytes_accessed=4 * nh * seq * hd * 2),
    )(q, k, v, lq, lk)


def attention_backward(q, k, v, do, labels, m, l, scale):
    nh, seq, hd = q.shape
    bq = min(BQ, seq)
    lq = labels.reshape(seq, 1)
    lk = labels.reshape(1, seq)
    grid = (nh, seq // bq)
    qspec = pl.BlockSpec((None, bq, hd), lambda h, i: (h, i, 0))
    kspec = pl.BlockSpec((None, seq, hd), lambda h, i: (h, 0, 0))
    rowspec = pl.BlockSpec((None, bq, 1), lambda h, i: (h, i, 0))
    flops = 10 * nh * seq * seq * hd
    return pl.pallas_call(
        functools.partial(_bwd_kernel, scale),
        grid=grid,
        in_specs=[qspec, kspec, kspec, qspec,
                  pl.BlockSpec((bq, 1), lambda h, i: (i, 0)),
                  pl.BlockSpec((1, seq), lambda h, i: (0, 0)),
                  rowspec, rowspec],
        out_specs=[qspec, kspec, kspec],
        out_shape=[jax.ShapeDtypeStruct((nh, seq, hd), jnp.bfloat16),
                   jax.ShapeDtypeStruct((nh, seq, hd), jnp.float32),
                   jax.ShapeDtypeStruct((nh, seq, hd), jnp.float32)],
        compiler_params=pltpu.CompilerParams(
            dimension_semantics=("parallel", "arbitrary"),
            vmem_limit_bytes=48 * 1024 * 1024),
        cost_estimate=pl.CostEstimate(flops=flops, transcendentals=nh * seq * seq,
                                      bytes_accessed=8 * nh * seq * hd * 2),
    )(q, k, v, do, lq, lk, m, l)


NORM_EPS = 1e-06


def feature_whole(blocked):
    return lax.all_gather(blocked, "col", axis=1, tiled=True)


def feature_sum(partial_rows):
    return lax.psum_scatter(partial_rows, "col", scatter_dimension=1, tiled=True)


def row_totals(first_term, second_term):
    return lax.psum((jnp.sum(first_term, axis=1), jnp.sum(second_term, axis=1)), "col")


def norm_forward(row_values, gain_row, shift_row):
    totals, squares = row_totals(row_values, row_values * row_values)
    mean_row = (totals / D)[:, None]
    var_row = (squares / D)[:, None] - mean_row * mean_row
    inverse = lax.rsqrt(var_row + NORM_EPS)
    normed = (row_values - mean_row) * inverse
    return (normed * gain_row + shift_row, normed, inverse)


def norm_backward(grad_rows, normed, inverse, gain_row):
    scaled = grad_rows * gain_row
    totals, along = row_totals(scaled, scaled * normed)
    back_rows = inverse * (scaled - (totals / D)[:, None] - normed * (along / D)[:, None])
    return (back_rows, jnp.sum(grad_rows * normed, axis=0), jnp.sum(grad_rows, axis=0))


def row_scatter_sum(partial_rows):
    count = lax.axis_size("row")
    me = lax.axis_index("row")
    blocks = partial_rows.reshape((count, partial_rows.shape[0] // count) + partial_rows.shape[1:])
    total = blocks[me]
    for shift in range(1, count):
        outgoing = blocks[lax.rem(me + shift, count)]
        total = total + lax.ppermute(
            outgoing, "row", [(i, (i + shift) % count) for i in range(count)]
        )
    return total


def row_sum(values):
    count = lax.axis_size("row")
    total = values
    for shift in range(1, count):
        total = total + lax.ppermute(
            values, "row", [(i, (i + shift) % count) for i in range(count)]
        )
    return total


def axis_gather(values, axis):
    count = lax.axis_size(axis)
    me = lax.axis_index(axis)
    arrived = [values]
    for shift in range(1, count):
        arrived.append(
            lax.ppermute(values, axis, [(i, (i + shift) % count) for i in range(count)])
        )
    order = lax.rem(me - jnp.arange(count) + count, count)
    return jnp.stack(arrived)[order]


def weight_partial(gathered, local_grad):
    return lax.dot_general(
        gathered, local_grad, (((0,), (0,)), ((), ())), preferred_element_type=jnp.float32
    )


def weight_grad(gathered, local_grad):
    return row_scatter_sum(
        lax.dot_general(
            gathered, local_grad, (((0,), (0,)), ((), ())), preferred_element_type=jnp.float32
        )
    )


def rows_gathered_many(blocks_and_axes):
    flat = jnp.concatenate([block.reshape(-1) for block, _ in blocks_and_axes])
    pieces = lax.all_gather(flat, "row", axis=0, tiled=False)
    wholes = []
    offset = 0
    for block, axis in blocks_and_axes:
        piece = pieces[:, offset : offset + block.size].reshape((-1,) + block.shape)
        offset += block.size
        piece = jnp.moveaxis(piece, 0, axis)
        shape = list(block.shape)
        shape[axis] = shape[axis] * piece.shape[axis]
        wholes.append(piece.reshape(shape))
    return wholes


def heads_major(rows, head_size):
    return rows.reshape(rows.shape[0], -1, head_size).transpose(1, 0, 2)


def heads_beside(stacked):
    return stacked.transpose(1, 0, 2).reshape(stacked.shape[1], -1)


def full_norm(row_values, gain_full, shift_full):
    mean_row = jnp.sum(row_values, axis=1, keepdims=True) / D
    var_row = jnp.sum(row_values * row_values, axis=1, keepdims=True) / D - mean_row * mean_row
    inverse = lax.rsqrt(var_row + NORM_EPS)
    normed = (row_values - mean_row) * inverse
    return (normed * gain_full + shift_full, normed, inverse)


def layer(
    inputs,
    segments,
    query_weight,
    key_weight,
    value_weight,
    query_bias,
    value_bias,
    output_weight,
    output_bias,
    attn_gain,
    attn_shift,
    up_weight,
    up_bias,
    down_weight,
    down_bias,
    final_gain,
    final_shift,
    cotangent,
):
    head_size = D // HEADS
    score_scale = head_size ** (-0.5)
    labels = segments[0]
    token_rows = inputs.T
    out_grad = cotangent.T.astype(jnp.float32)
    own_features = token_rows.shape[1]
    own_start = lax.axis_index("col") * own_features
    inputs_full = feature_whole(token_rows)
    qkv_stack = jnp.stack([query_weight, key_weight, value_weight])
    qkv_complete, output_rows = rows_gathered_many(((qkv_stack, 1), (output_weight, 1)))
    output_complete = lax.all_gather(output_rows, "col", axis=0, tiled=True)
    up_complete, down_complete = rows_gathered_many(((up_weight, 0), (down_weight, 1)))
    projected = jnp.einsum(
        "td,kdc->ktc", inputs_full, qkv_complete, preferred_element_type=jnp.float32
    )
    queries = heads_major((projected[0] + query_bias).astype(jnp.bfloat16), head_size)
    key_all = heads_major(projected[1].astype(jnp.bfloat16), head_size)
    value_all = heads_major((projected[2] + value_bias).astype(jnp.bfloat16), head_size)
    attended_h, row_max, row_total = attention_forward(
        queries, key_all, value_all, labels, score_scale
    )
    attended = heads_beside(attended_h)
    attended_full = feature_whole(attended)
    vectors_full = axis_gather(jnp.stack([output_bias, attn_gain, attn_shift]), "col")
    output_bias_full, gain_one_full, shift_one_full = (
        vectors_full[:, which].reshape(-1) for which in range(3)
    )
    first_sum_full = (
        inputs_full.astype(jnp.float32)
        + jnp.dot(attended_full, output_complete, preferred_element_type=jnp.float32)
        + output_bias_full
    )
    hidden_full_f, normed_one_full, inverse_one = full_norm(
        first_sum_full, gain_one_full, shift_one_full
    )
    hidden = lax.dynamic_slice_in_dim(hidden_full_f, own_start, own_features, axis=1)
    normed_one = lax.dynamic_slice_in_dim(normed_one_full, own_start, own_features, axis=1)
    hidden_full = hidden_full_f.astype(jnp.bfloat16)
    upped = jnp.dot(hidden_full, up_complete, preferred_element_type=jnp.float32) + up_bias
    acted_f, gelu_pull = jax.vjp(partial(jax.nn.gelu, approximate=False), upped)
    acted = acted_f.astype(jnp.bfloat16)
    ffn_partial = jnp.dot(acted, down_complete, preferred_element_type=jnp.float32)
    second_sum = hidden + feature_sum(ffn_partial) + down_bias
    result, normed_two, inverse_two = norm_forward(second_sum, final_gain, final_shift)
    second_grad, final_gain_grad, final_shift_grad = norm_backward(
        out_grad, normed_two, inverse_two, final_gain
    )
    branch_grad = second_grad.astype(jnp.bfloat16)
    branch_full = feature_whole(branch_grad)
    down_partial = weight_partial(branch_full, acted)
    acted_grad = lax.dot_general(
        branch_full, down_complete, (((1,), (1,)), ((), ())), preferred_element_type=jnp.float32
    )
    upped_grad = gelu_pull(acted_grad)[0].astype(jnp.bfloat16)
    up_partial = weight_partial(hidden_full, upped_grad)
    ffn_grads = row_scatter_sum(jnp.concatenate([down_partial, up_partial], axis=1))
    down_weight_grad = ffn_grads[:, : down_partial.shape[1]].T
    up_weight_grad = ffn_grads[:, down_partial.shape[1] :]
    hidden_grad = second_grad + feature_sum(
        lax.dot_general(
            upped_grad, up_complete, (((1,), (1,)), ((), ())), preferred_element_type=jnp.float32
        )
    )
    first_grad, attn_gain_grad, attn_shift_grad = norm_backward(
        hidden_grad, normed_one, inverse_one, attn_gain
    )
    attn_branch_grad = first_grad.astype(jnp.bfloat16)
    attn_branch_full = feature_whole(attn_branch_grad)
    output_weight_grad = weight_grad(attn_branch_full, attended).T
    attended_grad = lax.dot_general(
        attn_branch_full, output_rows, (((1,), (1,)), ((), ())), preferred_element_type=jnp.float32
    ).astype(jnp.bfloat16)
    query_grad_h, key_grad_h, value_grad_h = attention_backward(
        queries,
        key_all,
        value_all,
        heads_major(attended_grad, head_size),
        labels,
        row_max,
        row_total,
        score_scale,
    )
    query_grad = heads_beside(query_grad_h)
    key_grad = heads_beside(key_grad_h).astype(jnp.bfloat16)
    value_grad = heads_beside(value_grad_h).astype(jnp.bfloat16)
    column_count = query_weight.shape[1]
    qkv_grads = weight_grad(
        inputs_full, jnp.concatenate([query_grad, key_grad, value_grad], axis=1)
    )
    input_grad = first_grad + feature_sum(
        jnp.einsum(
            "ktc,kdc->td",
            jnp.stack([query_grad, key_grad, value_grad]),
            qkv_complete,
            preferred_element_type=jnp.float32,
        )
    )
    param_parts = (
        jnp.sum(query_grad.astype(jnp.float32), axis=0),
        jnp.sum(value_grad.astype(jnp.float32), axis=0),
        jnp.sum(attn_branch_grad.astype(jnp.float32), axis=0),
        attn_gain_grad,
        attn_shift_grad,
        jnp.sum(upped_grad.astype(jnp.float32), axis=0),
        jnp.sum(branch_grad.astype(jnp.float32), axis=0),
        final_gain_grad,
        final_shift_grad,
    )
    param_flat = row_sum(jnp.concatenate(param_parts))
    param_totals = []
    offset = 0
    for part in param_parts:
        param_totals.append(param_flat[offset : offset + part.shape[0]])
        offset += part.shape[0]
    return (
        result.astype(jnp.bfloat16).T,
        input_grad.astype(jnp.bfloat16).T,
        qkv_grads[:, :column_count],
        qkv_grads[:, column_count : 2 * column_count],
        qkv_grads[:, 2 * column_count :],
        param_totals[0],
        param_totals[1],
        output_weight_grad,
        param_totals[2],
        param_totals[3],
        param_totals[4],
        up_weight_grad,
        param_totals[5],
        down_weight_grad,
        param_totals[6],
        param_totals[7],
        param_totals[8],
    )


def solution(mesh):
    placed = (
        P("col", "row"),
        P("row", None),
        P("row", "col"),
        P("row", "col"),
        P("row", "col"),
        P("col"),
        P("col"),
        P("col", "row"),
        P("col"),
        P("col"),
        P("col"),
        P("row", "col"),
        P("col"),
        P("col", "row"),
        P("col"),
        P("col"),
        P("col"),
        P("col", "row"),
    )
    return jax.shard_map(
        layer,
        mesh=mesh,
        in_specs=placed,
        out_specs=(
            P("col", "row"),
            P("col", "row"),
            P("row", "col"),
            P("row", "col"),
            P("row", "col"),
            P("col"),
            P("col"),
            P("col", "row"),
            P("col"),
            P("col"),
            P("col"),
            P("row", "col"),
            P("col"),
            P("col", "row"),
            P("col"),
            P("col"),
            P("col"),
        ),
        check_vma=False,
    )
```

```python
from functools import partial
import functools

import jax
import jax.numpy as jnp
from jax import lax
from jax.experimental import pallas as pl
from jax.experimental.pallas import tpu as pltpu
from jax.sharding import PartitionSpec as P

D = 768
HEADS = 12
BQ = 256


def _mask(lab_q, lab_k, q0, bq, nk):
    rows = q0 + lax.broadcasted_iota(jnp.int32, (bq, nk), 0)
    cols = lax.broadcasted_iota(jnp.int32, (bq, nk), 1)
    return ((lab_q == lab_k) & (lab_k > 0)) | (rows == cols)


def _fwd_kernel(scale, q_ref, k_ref, v_ref, lq_ref, lk_ref, o_ref, m_ref, l_ref):
    i = pl.program_id(1)
    bq = q_ref.shape[0]
    nk = k_ref.shape[0]
    s = lax.dot_general(q_ref[...], k_ref[...], (((1,), (1,)), ((), ())),
                        preferred_element_type=jnp.float32) * scale
    allowed = _mask(lq_ref[...], lk_ref[...], i * bq, bq, nk)
    s = jnp.where(allowed, s, -1000000000.0)
    m = jnp.max(s, axis=1, keepdims=True)
    e = jnp.exp(s - m)
    l = jnp.sum(e, axis=1, keepdims=True)
    p = (e / l).astype(jnp.bfloat16)
    o_ref[...] = jnp.dot(p, v_ref[...], preferred_element_type=jnp.float32).astype(o_ref.dtype)
    m_ref[...] = m
    l_ref[...] = l


def _bwd_kernel(scale, q_ref, k_ref, v_ref, do_ref, lq_ref, lk_ref, m_ref, l_ref,
                dq_ref, dk_ref, dv_ref):
    i = pl.program_id(1)
    bq = q_ref.shape[0]
    nk = k_ref.shape[0]

    @pl.when(i == 0)
    def _():
        dk_ref[...] = jnp.zeros_like(dk_ref)
        dv_ref[...] = jnp.zeros_like(dv_ref)

    q = q_ref[...]
    k = k_ref[...]
    s = lax.dot_general(q, k, (((1,), (1,)), ((), ())),
                        preferred_element_type=jnp.float32) * scale
    allowed = _mask(lq_ref[...], lk_ref[...], i * bq, bq, nk)
    s = jnp.where(allowed, s, -1000000000.0)
    p = jnp.where(allowed, jnp.exp(s - m_ref[...]) / l_ref[...], 0.0)
    do = do_ref[...]
    dp = lax.dot_general(do, v_ref[...], (((1,), (1,)), ((), ())),
                         preferred_element_type=jnp.float32)
    inner = jnp.sum(p * dp, axis=1, keepdims=True)
    ds = (p * (dp - inner)).astype(jnp.bfloat16)
    dq_ref[...] = (jnp.dot(ds, k, preferred_element_type=jnp.float32) * scale).astype(dq_ref.dtype)
    dk_ref[...] += lax.dot_general(ds, q, (((0,), (0,)), ((), ())),
                                   preferred_element_type=jnp.float32) * scale
    dv_ref[...] += lax.dot_general(p.astype(jnp.bfloat16), do, (((0,), (0,)), ((), ())),
                                   preferred_element_type=jnp.float32)


def attention_forward(q, k, v, labels, scale):
    nh, seq, hd = q.shape
    bq = min(BQ, seq)
    lq = labels.reshape(seq, 1)
    lk = labels.reshape(1, seq)
    grid = (nh, seq // bq)
    qspec = pl.BlockSpec((None, bq, hd), lambda h, i: (h, i, 0))
    kspec = pl.BlockSpec((None, seq, hd), lambda h, i: (h, 0, 0))
    rowspec = pl.BlockSpec((None, bq, 1), lambda h, i: (h, i, 0))
    flops = 4 * nh * seq * seq * hd
    return pl.pallas_call(
        functools.partial(_fwd_kernel, scale),
        grid=grid,
        in_specs=[qspec, kspec, kspec,
                  pl.BlockSpec((bq, 1), lambda h, i: (i, 0)),
                  pl.BlockSpec((1, seq), lambda h, i: (0, 0))],
        out_specs=[qspec, rowspec, rowspec],
        out_shape=[jax.ShapeDtypeStruct((nh, seq, hd), jnp.bfloat16),
                   jax.ShapeDtypeStruct((nh, seq, 1), jnp.float32),
                   jax.ShapeDtypeStruct((nh, seq, 1), jnp.float32)],
        compiler_params=pltpu.CompilerParams(
            dimension_semantics=("parallel", "arbitrary"),
            vmem_limit_bytes=48 * 1024 * 1024),
        cost_estimate=pl.CostEstimate(flops=flops, transcendentals=nh * seq * seq,
                                      bytes_accessed=4 * nh * seq * hd * 2),
    )(q, k, v, lq, lk)


def attention_backward(q, k, v, do, labels, m, l, scale):
    nh, seq, hd = q.shape
    bq = min(BQ, seq)
    lq = labels.reshape(seq, 1)
    lk = labels.reshape(1, seq)
    grid = (nh, seq // bq)
    qspec = pl.BlockSpec((None, bq, hd), lambda h, i: (h, i, 0))
    kspec = pl.BlockSpec((None, seq, hd), lambda h, i: (h, 0, 0))
    rowspec = pl.BlockSpec((None, bq, 1), lambda h, i: (h, i, 0))
    flops = 10 * nh * seq * seq * hd
    return pl.pallas_call(
        functools.partial(_bwd_kernel, scale),
        grid=grid,
        in_specs=[qspec, kspec, kspec, qspec,
                  pl.BlockSpec((bq, 1), lambda h, i: (i, 0)),
                  pl.BlockSpec((1, seq), lambda h, i: (0, 0)),
                  rowspec, rowspec],
        out_specs=[qspec, kspec, kspec],
        out_shape=[jax.ShapeDtypeStruct((nh, seq, hd), jnp.bfloat16),
                   jax.ShapeDtypeStruct((nh, seq, hd), jnp.float32),
                   jax.ShapeDtypeStruct((nh, seq, hd), jnp.float32)],
        compiler_params=pltpu.CompilerParams(
            dimension_semantics=("parallel", "arbitrary"),
            vmem_limit_bytes=48 * 1024 * 1024),
        cost_estimate=pl.CostEstimate(flops=flops, transcendentals=nh * seq * seq,
                                      bytes_accessed=8 * nh * seq * hd * 2),
    )(q, k, v, do, lq, lk, m, l)


NORM_EPS = 1e-06


def feature_whole_sent(blocked):
    pieces = axis_gather(blocked, "col")
    return jnp.moveaxis(pieces, 0, 1).reshape(blocked.shape[0], -1)


def feature_sum(partial_rows):
    return lax.psum_scatter(partial_rows, "col", scatter_dimension=1, tiled=True)


def row_totals(first_term, second_term):
    return lax.psum((jnp.sum(first_term, axis=1), jnp.sum(second_term, axis=1)), "col")


def norm_forward(row_values, gain_row, shift_row):
    totals, squares = row_totals(row_values, row_values * row_values)
    mean_row = (totals / D)[:, None]
    var_row = (squares / D)[:, None] - mean_row * mean_row
    inverse = lax.rsqrt(var_row + NORM_EPS)
    normed = (row_values - mean_row) * inverse
    return (normed * gain_row + shift_row, normed, inverse)


def norm_backward(grad_rows, normed, inverse, gain_row):
    scaled = grad_rows * gain_row
    totals, along = row_totals(scaled, scaled * normed)
    back_rows = inverse * (scaled - (totals / D)[:, None] - normed * (along / D)[:, None])
    return (back_rows, jnp.sum(grad_rows * normed, axis=0), jnp.sum(grad_rows, axis=0))


def row_scatter_sum(partial_rows):
    count = lax.axis_size("row")
    me = lax.axis_index("row")
    blocks = partial_rows.reshape((count, partial_rows.shape[0] // count) + partial_rows.shape[1:])
    total = blocks[me]
    for shift in range(1, count):
        outgoing = blocks[lax.rem(me + shift, count)]
        total = total + lax.ppermute(
            outgoing, "row", [(i, (i + shift) % count) for i in range(count)]
        )
    return total


def row_sum(values):
    count = lax.axis_size("row")
    total = values
    for shift in range(1, count):
        total = total + lax.ppermute(
            values, "row", [(i, (i + shift) % count) for i in range(count)]
        )
    return total


def axis_gather(values, axis):
    count = lax.axis_size(axis)
    me = lax.axis_index(axis)
    arrived = [values]
    for shift in range(1, count):
        arrived.append(
            lax.ppermute(values, axis, [(i, (i + shift) % count) for i in range(count)])
        )
    order = lax.rem(me - jnp.arange(count) + count, count)
    return jnp.stack(arrived)[order]


def weight_partial(gathered, local_grad):
    return lax.dot_general(
        gathered, local_grad, (((0,), (0,)), ((), ())), preferred_element_type=jnp.float32
    )


def weight_grad(gathered, local_grad):
    return row_scatter_sum(
        lax.dot_general(
            gathered, local_grad, (((0,), (0,)), ((), ())), preferred_element_type=jnp.float32
        )
    )


def rows_gathered_many(blocks_and_axes, sent=False):
    flat = jnp.concatenate([block.reshape(-1) for block, _ in blocks_and_axes])
    if sent:
        pieces = axis_gather(flat, "row")
    else:
        pieces = lax.all_gather(flat, "row", axis=0, tiled=False)
    wholes = []
    offset = 0
    for block, axis in blocks_and_axes:
        piece = pieces[:, offset : offset + block.size].reshape((-1,) + block.shape)
        offset += block.size
        piece = jnp.moveaxis(piece, 0, axis)
        shape = list(block.shape)
        shape[axis] = shape[axis] * piece.shape[axis]
        wholes.append(piece.reshape(shape))
    return wholes


def heads_major(rows, head_size):
    return rows.reshape(rows.shape[0], -1, head_size).transpose(1, 0, 2)


def heads_beside(stacked):
    return stacked.transpose(1, 0, 2).reshape(stacked.shape[1], -1)


def full_norm(row_values, gain_full, shift_full):
    mean_row = jnp.sum(row_values, axis=1, keepdims=True) / D
    var_row = jnp.sum(row_values * row_values, axis=1, keepdims=True) / D - mean_row * mean_row
    inverse = lax.rsqrt(var_row + NORM_EPS)
    normed = (row_values - mean_row) * inverse
    return (normed * gain_full + shift_full, normed, inverse)


def layer(
    inputs,
    segments,
    query_weight,
    key_weight,
    value_weight,
    query_bias,
    value_bias,
    output_weight,
    output_bias,
    attn_gain,
    attn_shift,
    up_weight,
    up_bias,
    down_weight,
    down_bias,
    final_gain,
    final_shift,
    cotangent,
):
    head_size = D // HEADS
    score_scale = head_size ** (-0.5)
    labels = segments[0]
    token_rows = inputs.T
    out_grad = cotangent.T.astype(jnp.float32)
    own_features = token_rows.shape[1]
    own_start = lax.axis_index("col") * own_features
    inputs_full = axis_gather(inputs, "col").reshape(-1, inputs.shape[1]).T
    qkv_stack = jnp.stack([query_weight, key_weight, value_weight])
    qkv_complete, output_rows = rows_gathered_many(((qkv_stack, 1), (output_weight, 1)), sent=True)
    output_complete = lax.all_gather(output_rows, "col", axis=0, tiled=True)
    up_complete, down_complete = rows_gathered_many(((up_weight, 0), (down_weight, 1)))
    projected = jnp.einsum(
        "td,kdc->ktc", inputs_full, qkv_complete, preferred_element_type=jnp.float32
    )
    queries = heads_major((projected[0] + query_bias).astype(jnp.bfloat16), head_size)
    key_all = heads_major(projected[1].astype(jnp.bfloat16), head_size)
    value_all = heads_major((projected[2] + value_bias).astype(jnp.bfloat16), head_size)
    attended_h, row_max, row_total = attention_forward(
        queries, key_all, value_all, labels, score_scale
    )
    attended = heads_beside(attended_h)
    attended_full = feature_whole_sent(attended)
    vectors_full = axis_gather(jnp.stack([output_bias, attn_gain, attn_shift]), "col")
    output_bias_full, gain_one_full, shift_one_full = (
        vectors_full[:, which].reshape(-1) for which in range(3)
    )
    first_sum_full = (
        inputs_full.astype(jnp.float32)
        + jnp.dot(attended_full, output_complete, preferred_element_type=jnp.float32)
        + output_bias_full
    )
    hidden_full_f, normed_one_full, inverse_one = full_norm(
        first_sum_full, gain_one_full, shift_one_full
    )
    hidden = lax.dynamic_slice_in_dim(hidden_full_f, own_start, own_features, axis=1)
    normed_one = lax.dynamic_slice_in_dim(normed_one_full, own_start, own_features, axis=1)
    hidden_full = hidden_full_f.astype(jnp.bfloat16)
    upped = jnp.dot(hidden_full, up_complete, preferred_element_type=jnp.float32) + up_bias
    acted_f, gelu_pull = jax.vjp(partial(jax.nn.gelu, approximate=False), upped)
    acted = acted_f.astype(jnp.bfloat16)
    ffn_partial = jnp.dot(acted, down_complete, preferred_element_type=jnp.float32)
    second_sum = hidden + feature_sum(ffn_partial) + down_bias
    result, normed_two, inverse_two = norm_forward(second_sum, final_gain, final_shift)
    second_grad, final_gain_grad, final_shift_grad = norm_backward(
        out_grad, normed_two, inverse_two, final_gain
    )
    branch_grad = second_grad.astype(jnp.bfloat16)
    branch_full = feature_whole_sent(branch_grad)
    down_partial = weight_partial(branch_full, acted)
    acted_grad = lax.dot_general(
        branch_full, down_complete, (((1,), (1,)), ((), ())), preferred_element_type=jnp.float32
    )
    upped_grad = gelu_pull(acted_grad)[0].astype(jnp.bfloat16)
    up_partial = weight_partial(hidden_full, upped_grad)
    ffn_grads = row_scatter_sum(jnp.concatenate([down_partial, up_partial], axis=1))
    down_weight_grad = ffn_grads[:, : down_partial.shape[1]].T
    up_weight_grad = ffn_grads[:, down_partial.shape[1] :]
    hidden_grad = second_grad + feature_sum(
        lax.dot_general(
            upped_grad, up_complete, (((1,), (1,)), ((), ())), preferred_element_type=jnp.float32
        )
    )
    first_grad, attn_gain_grad, attn_shift_grad = norm_backward(
        hidden_grad, normed_one, inverse_one, attn_gain
    )
    attn_branch_grad = first_grad.astype(jnp.bfloat16)
    attn_branch_full = feature_whole_sent(attn_branch_grad)
    output_weight_grad = weight_grad(attn_branch_full, attended).T
    attended_grad = lax.dot_general(
        attn_branch_full, output_rows, (((1,), (1,)), ((), ())), preferred_element_type=jnp.float32
    ).astype(jnp.bfloat16)
    query_grad_h, key_grad_h, value_grad_h = attention_backward(
        queries,
        key_all,
        value_all,
        heads_major(attended_grad, head_size),
        labels,
        row_max,
        row_total,
        score_scale,
    )
    query_grad = heads_beside(query_grad_h)
    key_grad = heads_beside(key_grad_h).astype(jnp.bfloat16)
    value_grad = heads_beside(value_grad_h).astype(jnp.bfloat16)
    column_count = query_weight.shape[1]
    qkv_grads = weight_grad(
        inputs_full, jnp.concatenate([query_grad, key_grad, value_grad], axis=1)
    )
    input_grad = first_grad + feature_sum(
        jnp.einsum(
            "ktc,kdc->td",
            jnp.stack([query_grad, key_grad, value_grad]),
            qkv_complete,
            preferred_element_type=jnp.float32,
        )
    )
    param_parts = (
        jnp.sum(query_grad.astype(jnp.float32), axis=0),
        jnp.sum(value_grad.astype(jnp.float32), axis=0),
        jnp.sum(attn_branch_grad.astype(jnp.float32), axis=0),
        attn_gain_grad,
        attn_shift_grad,
        jnp.sum(upped_grad.astype(jnp.float32), axis=0),
        jnp.sum(branch_grad.astype(jnp.float32), axis=0),
        final_gain_grad,
        final_shift_grad,
    )
    param_flat = row_sum(jnp.concatenate(param_parts))
    param_totals = []
    offset = 0
    for part in param_parts:
        param_totals.append(param_flat[offset : offset + part.shape[0]])
        offset += part.shape[0]
    return (
        result.astype(jnp.bfloat16).T,
        input_grad.astype(jnp.bfloat16).T,
        qkv_grads[:, :column_count],
        qkv_grads[:, column_count : 2 * column_count],
        qkv_grads[:, 2 * column_count :],
        param_totals[0],
        param_totals[1],
        output_weight_grad,
        param_totals[2],
        param_totals[3],
        param_totals[4],
        up_weight_grad,
        param_totals[5],
        down_weight_grad,
        param_totals[6],
        param_totals[7],
        param_totals[8],
    )


def solution(mesh):
    placed = (
        P("col", "row"),
        P("row", None),
        P("row", "col"),
        P("row", "col"),
        P("row", "col"),
        P("col"),
        P("col"),
        P("col", "row"),
        P("col"),
        P("col"),
        P("col"),
        P("row", "col"),
        P("col"),
        P("col", "row"),
        P("col"),
        P("col"),
        P("col"),
        P("col", "row"),
    )
    return jax.shard_map(
        layer,
        mesh=mesh,
        in_specs=placed,
        out_specs=(
            P("col", "row"),
            P("col", "row"),
            P("row", "col"),
            P("row", "col"),
            P("row", "col"),
            P("col"),
            P("col"),
            P("col", "row"),
            P("col"),
            P("col"),
            P("col"),
            P("row", "col"),
            P("col"),
            P("col", "row"),
            P("col"),
            P("col"),
            P("col"),
        ),
        check_vma=False,
    )
```

```python
from functools import partial
import functools

import jax
import jax.numpy as jnp
from jax import lax
from jax.experimental import pallas as pl
from jax.experimental.pallas import tpu as pltpu
from jax.sharding import PartitionSpec as P

D = 768
HEADS = 12
BQ = 256


def _mask(lab_q, lab_k, q0, bq, nk):
    rows = q0 + lax.broadcasted_iota(jnp.int32, (bq, nk), 0)
    cols = lax.broadcasted_iota(jnp.int32, (bq, nk), 1)
    return ((lab_q == lab_k) & (lab_k > 0)) | (rows == cols)


def _fwd_kernel(scale, q_ref, k_ref, v_ref, lq_ref, lk_ref, o_ref, m_ref, l_ref):
    i = pl.program_id(1)
    bq = q_ref.shape[0]
    nk = k_ref.shape[0]
    s = lax.dot_general(q_ref[...], k_ref[...], (((1,), (1,)), ((), ())),
                        preferred_element_type=jnp.float32) * scale
    allowed = _mask(lq_ref[...], lk_ref[...], i * bq, bq, nk)
    s = jnp.where(allowed, s, -1000000000.0)
    m = jnp.max(s, axis=1, keepdims=True)
    e = jnp.exp(s - m)
    l = jnp.sum(e, axis=1, keepdims=True)
    p = (e / l).astype(jnp.bfloat16)
    o_ref[...] = jnp.dot(p, v_ref[...], preferred_element_type=jnp.float32).astype(o_ref.dtype)
    m_ref[...] = m
    l_ref[...] = l


def _bwd_kernel(scale, q_ref, k_ref, v_ref, do_ref, lq_ref, lk_ref, m_ref, l_ref,
                dq_ref, dk_ref, dv_ref):
    i = pl.program_id(1)
    bq = q_ref.shape[0]
    nk = k_ref.shape[0]

    @pl.when(i == 0)
    def _():
        dk_ref[...] = jnp.zeros_like(dk_ref)
        dv_ref[...] = jnp.zeros_like(dv_ref)

    q = q_ref[...]
    k = k_ref[...]
    s = lax.dot_general(q, k, (((1,), (1,)), ((), ())),
                        preferred_element_type=jnp.float32) * scale
    allowed = _mask(lq_ref[...], lk_ref[...], i * bq, bq, nk)
    s = jnp.where(allowed, s, -1000000000.0)
    p = jnp.where(allowed, jnp.exp(s - m_ref[...]) / l_ref[...], 0.0)
    do = do_ref[...]
    dp = lax.dot_general(do, v_ref[...], (((1,), (1,)), ((), ())),
                         preferred_element_type=jnp.float32)
    inner = jnp.sum(p * dp, axis=1, keepdims=True)
    ds = (p * (dp - inner)).astype(jnp.bfloat16)
    dq_ref[...] = (jnp.dot(ds, k, preferred_element_type=jnp.float32) * scale).astype(dq_ref.dtype)
    dk_ref[...] += lax.dot_general(ds, q, (((0,), (0,)), ((), ())),
                                   preferred_element_type=jnp.float32) * scale
    dv_ref[...] += lax.dot_general(p.astype(jnp.bfloat16), do, (((0,), (0,)), ((), ())),
                                   preferred_element_type=jnp.float32)


def attention_forward(q, k, v, labels, scale):
    nh, seq, hd = q.shape
    bq = min(BQ, seq)
    lq = labels.reshape(seq, 1)
    lk = labels.reshape(1, seq)
    grid = (nh, seq // bq)
    qspec = pl.BlockSpec((None, bq, hd), lambda h, i: (h, i, 0))
    kspec = pl.BlockSpec((None, seq, hd), lambda h, i: (h, 0, 0))
    rowspec = pl.BlockSpec((None, bq, 1), lambda h, i: (h, i, 0))
    flops = 4 * nh * seq * seq * hd
    return pl.pallas_call(
        functools.partial(_fwd_kernel, scale),
        grid=grid,
        in_specs=[qspec, kspec, kspec,
                  pl.BlockSpec((bq, 1), lambda h, i: (i, 0)),
                  pl.BlockSpec((1, seq), lambda h, i: (0, 0))],
        out_specs=[qspec, rowspec, rowspec],
        out_shape=[jax.ShapeDtypeStruct((nh, seq, hd), jnp.bfloat16),
                   jax.ShapeDtypeStruct((nh, seq, 1), jnp.float32),
                   jax.ShapeDtypeStruct((nh, seq, 1), jnp.float32)],
        compiler_params=pltpu.CompilerParams(
            dimension_semantics=("parallel", "arbitrary"),
            vmem_limit_bytes=48 * 1024 * 1024),
        cost_estimate=pl.CostEstimate(flops=flops, transcendentals=nh * seq * seq,
                                      bytes_accessed=4 * nh * seq * hd * 2),
    )(q, k, v, lq, lk)


def attention_backward(q, k, v, do, labels, m, l, scale):
    nh, seq, hd = q.shape
    bq = min(BQ, seq)
    lq = labels.reshape(seq, 1)
    lk = labels.reshape(1, seq)
    grid = (nh, seq // bq)
    qspec = pl.BlockSpec((None, bq, hd), lambda h, i: (h, i, 0))
    kspec = pl.BlockSpec((None, seq, hd), lambda h, i: (h, 0, 0))
    rowspec = pl.BlockSpec((None, bq, 1), lambda h, i: (h, i, 0))
    flops = 10 * nh * seq * seq * hd
    return pl.pallas_call(
        functools.partial(_bwd_kernel, scale),
        grid=grid,
        in_specs=[qspec, kspec, kspec, qspec,
                  pl.BlockSpec((bq, 1), lambda h, i: (i, 0)),
                  pl.BlockSpec((1, seq), lambda h, i: (0, 0)),
                  rowspec, rowspec],
        out_specs=[qspec, kspec, kspec],
        out_shape=[jax.ShapeDtypeStruct((nh, seq, hd), jnp.bfloat16),
                   jax.ShapeDtypeStruct((nh, seq, hd), jnp.float32),
                   jax.ShapeDtypeStruct((nh, seq, hd), jnp.float32)],
        compiler_params=pltpu.CompilerParams(
            dimension_semantics=("parallel", "arbitrary"),
            vmem_limit_bytes=48 * 1024 * 1024),
        cost_estimate=pl.CostEstimate(flops=flops, transcendentals=nh * seq * seq,
                                      bytes_accessed=8 * nh * seq * hd * 2),
    )(q, k, v, do, lq, lk, m, l)


NORM_EPS = 1e-06


def feature_whole(blocked):
    return lax.all_gather(blocked, "col", axis=1, tiled=True)


def feature_sum(partial_rows):
    return lax.psum_scatter(
        partial_rows.astype(jnp.bfloat16), "col", scatter_dimension=1, tiled=True
    ).astype(jnp.float32)


def row_totals(first_term, second_term):
    return lax.psum((jnp.sum(first_term, axis=1), jnp.sum(second_term, axis=1)), "col")


def norm_forward(row_values, gain_row, shift_row):
    totals, squares = row_totals(row_values, row_values * row_values)
    mean_row = (totals / D)[:, None]
    var_row = (squares / D)[:, None] - mean_row * mean_row
    inverse = lax.rsqrt(var_row + NORM_EPS)
    normed = (row_values - mean_row) * inverse
    return (normed * gain_row + shift_row, normed, inverse)


def norm_backward(grad_rows, normed, inverse, gain_row):
    scaled = grad_rows * gain_row
    totals, along = row_totals(scaled, scaled * normed)
    back_rows = inverse * (scaled - (totals / D)[:, None] - normed * (along / D)[:, None])
    return (back_rows, jnp.sum(grad_rows * normed, axis=0), jnp.sum(grad_rows, axis=0))


def row_scatter_sum(partial_rows):
    count = lax.axis_size("row")
    me = lax.axis_index("row")
    blocks = partial_rows.reshape((count, partial_rows.shape[0] // count) + partial_rows.shape[1:])
    total = blocks[me]
    for shift in range(1, count):
        outgoing = blocks[lax.rem(me + shift, count)]
        total = total + lax.ppermute(
            outgoing, "row", [(i, (i + shift) % count) for i in range(count)]
        )
    return total


def row_sum(values):
    count = lax.axis_size("row")
    total = values
    for shift in range(1, count):
        total = total + lax.ppermute(
            values, "row", [(i, (i + shift) % count) for i in range(count)]
        )
    return total


def axis_gather(values, axis):
    count = lax.axis_size(axis)
    me = lax.axis_index(axis)
    arrived = [values]
    for shift in range(1, count):
        arrived.append(
            lax.ppermute(values, axis, [(i, (i + shift) % count) for i in range(count)])
        )
    order = lax.rem(me - jnp.arange(count) + count, count)
    return jnp.stack(arrived)[order]


def weight_partial(gathered, local_grad):
    return lax.dot_general(
        gathered, local_grad, (((0,), (0,)), ((), ())), preferred_element_type=jnp.float32
    )


def weight_grad(gathered, local_grad):
    return row_scatter_sum(
        lax.dot_general(
            gathered, local_grad, (((0,), (0,)), ((), ())), preferred_element_type=jnp.float32
        )
    )


def rows_gathered_many(blocks_and_axes, sent=False):
    flat = jnp.concatenate([block.reshape(-1) for block, _ in blocks_and_axes])
    if sent:
        pieces = axis_gather(flat, "row")
    else:
        pieces = lax.all_gather(flat, "row", axis=0, tiled=False)
    wholes = []
    offset = 0
    for block, axis in blocks_and_axes:
        piece = pieces[:, offset : offset + block.size].reshape((-1,) + block.shape)
        offset += block.size
        piece = jnp.moveaxis(piece, 0, axis)
        shape = list(block.shape)
        shape[axis] = shape[axis] * piece.shape[axis]
        wholes.append(piece.reshape(shape))
    return wholes


def heads_major(rows, head_size):
    return rows.reshape(rows.shape[0], -1, head_size).transpose(1, 0, 2)


def heads_beside(stacked):
    return stacked.transpose(1, 0, 2).reshape(stacked.shape[1], -1)


def full_norm(row_values, gain_full, shift_full):
    mean_row = jnp.sum(row_values, axis=1, keepdims=True) / D
    var_row = jnp.sum(row_values * row_values, axis=1, keepdims=True) / D - mean_row * mean_row
    inverse = lax.rsqrt(var_row + NORM_EPS)
    normed = (row_values - mean_row) * inverse
    return (normed * gain_full + shift_full, normed, inverse)


def layer(
    inputs,
    segments,
    query_weight,
    key_weight,
    value_weight,
    query_bias,
    value_bias,
    output_weight,
    output_bias,
    attn_gain,
    attn_shift,
    up_weight,
    up_bias,
    down_weight,
    down_bias,
    final_gain,
    final_shift,
    cotangent,
):
    head_size = D // HEADS
    score_scale = head_size ** (-0.5)
    labels = segments[0]
    token_rows = inputs.T
    out_grad = cotangent.T.astype(jnp.float32)
    own_features = token_rows.shape[1]
    own_start = lax.axis_index("col") * own_features
    inputs_full = axis_gather(inputs, "col").reshape(-1, inputs.shape[1]).T
    qkv_stack = jnp.stack([query_weight, key_weight, value_weight])
    qkv_complete, output_rows = rows_gathered_many(((qkv_stack, 1), (output_weight, 1)), sent=True)
    output_complete = lax.all_gather(output_rows, "col", axis=0, tiled=True)
    up_complete, down_complete = rows_gathered_many(((up_weight, 0), (down_weight, 1)))
    projected = jnp.einsum(
        "td,kdc->ktc", inputs_full, qkv_complete, preferred_element_type=jnp.float32
    )
    queries = heads_major((projected[0] + query_bias).astype(jnp.bfloat16), head_size)
    key_all = heads_major(projected[1].astype(jnp.bfloat16), head_size)
    value_all = heads_major((projected[2] + value_bias).astype(jnp.bfloat16), head_size)
    attended_h, row_max, row_total = attention_forward(
        queries, key_all, value_all, labels, score_scale
    )
    attended = heads_beside(attended_h)
    attended_full = feature_whole(attended)
    vectors_full = axis_gather(jnp.stack([output_bias, attn_gain, attn_shift]), "col")
    output_bias_full, gain_one_full, shift_one_full = (
        vectors_full[:, which].reshape(-1) for which in range(3)
    )
    first_sum_full = (
        inputs_full.astype(jnp.float32)
        + jnp.dot(attended_full, output_complete, preferred_element_type=jnp.float32)
        + output_bias_full
    )
    hidden_full_f, normed_one_full, inverse_one = full_norm(
        first_sum_full, gain_one_full, shift_one_full
    )
    hidden = lax.dynamic_slice_in_dim(hidden_full_f, own_start, own_features, axis=1)
    normed_one = lax.dynamic_slice_in_dim(normed_one_full, own_start, own_features, axis=1)
    hidden_full = hidden_full_f.astype(jnp.bfloat16)
    upped = jnp.dot(hidden_full, up_complete, preferred_element_type=jnp.float32) + up_bias
    acted_f, gelu_pull = jax.vjp(partial(jax.nn.gelu, approximate=False), upped)
    acted = acted_f.astype(jnp.bfloat16)
    ffn_partial = jnp.dot(acted, down_complete, preferred_element_type=jnp.float32)
    second_sum = hidden + feature_sum(ffn_partial) + down_bias
    result, normed_two, inverse_two = norm_forward(second_sum, final_gain, final_shift)
    second_grad, final_gain_grad, final_shift_grad = norm_backward(
        out_grad, normed_two, inverse_two, final_gain
    )
    branch_grad = second_grad.astype(jnp.bfloat16)
    branch_full = feature_whole(branch_grad)
    down_partial = weight_partial(branch_full, acted)
    acted_grad = lax.dot_general(
        branch_full, down_complete, (((1,), (1,)), ((), ())), preferred_element_type=jnp.float32
    )
    upped_grad = gelu_pull(acted_grad)[0].astype(jnp.bfloat16)
    up_partial = weight_partial(hidden_full, upped_grad)
    ffn_grads = row_scatter_sum(jnp.concatenate([down_partial, up_partial], axis=1))
    down_weight_grad = ffn_grads[:, : down_partial.shape[1]].T
    up_weight_grad = ffn_grads[:, down_partial.shape[1] :]
    hidden_grad = second_grad + feature_sum(
        lax.dot_general(
            upped_grad, up_complete, (((1,), (1,)), ((), ())), preferred_element_type=jnp.float32
        )
    )
    first_grad, attn_gain_grad, attn_shift_grad = norm_backward(
        hidden_grad, normed_one, inverse_one, attn_gain
    )
    attn_branch_grad = first_grad.astype(jnp.bfloat16)
    attn_branch_full = feature_whole(attn_branch_grad)
    output_weight_grad = weight_grad(attn_branch_full, attended).T
    attended_grad = lax.dot_general(
        attn_branch_full, output_rows, (((1,), (1,)), ((), ())), preferred_element_type=jnp.float32
    ).astype(jnp.bfloat16)
    query_grad_h, key_grad_h, value_grad_h = attention_backward(
        queries,
        key_all,
        value_all,
        heads_major(attended_grad, head_size),
        labels,
        row_max,
        row_total,
        score_scale,
    )
    query_grad = heads_beside(query_grad_h)
    key_grad = heads_beside(key_grad_h).astype(jnp.bfloat16)
    value_grad = heads_beside(value_grad_h).astype(jnp.bfloat16)
    column_count = query_weight.shape[1]
    qkv_grads = weight_grad(
        inputs_full, jnp.concatenate([query_grad, key_grad, value_grad], axis=1)
    )
    input_grad = first_grad + feature_sum(
        jnp.einsum(
            "ktc,kdc->td",
            jnp.stack([query_grad, key_grad, value_grad]),
            qkv_complete,
            preferred_element_type=jnp.float32,
        )
    )
    param_parts = (
        jnp.sum(query_grad.astype(jnp.float32), axis=0),
        jnp.sum(value_grad.astype(jnp.float32), axis=0),
        jnp.sum(attn_branch_grad.astype(jnp.float32), axis=0),
        attn_gain_grad,
        attn_shift_grad,
        jnp.sum(upped_grad.astype(jnp.float32), axis=0),
        jnp.sum(branch_grad.astype(jnp.float32), axis=0),
        final_gain_grad,
        final_shift_grad,
    )
    param_flat = row_sum(jnp.concatenate(param_parts))
    param_totals = []
    offset = 0
    for part in param_parts:
        param_totals.append(param_flat[offset : offset + part.shape[0]])
        offset += part.shape[0]
    return (
        result.astype(jnp.bfloat16).T,
        input_grad.astype(jnp.bfloat16).T,
        qkv_grads[:, :column_count],
        qkv_grads[:, column_count : 2 * column_count],
        qkv_grads[:, 2 * column_count :],
        param_totals[0],
        param_totals[1],
        output_weight_grad,
        param_totals[2],
        param_totals[3],
        param_totals[4],
        up_weight_grad,
        param_totals[5],
        down_weight_grad,
        param_totals[6],
        param_totals[7],
        param_totals[8],
    )


def solution(mesh):
    placed = (
        P("col", "row"),
        P("row", None),
        P("row", "col"),
        P("row", "col"),
        P("row", "col"),
        P("col"),
        P("col"),
        P("col", "row"),
        P("col"),
        P("col"),
        P("col"),
        P("row", "col"),
        P("col"),
        P("col", "row"),
        P("col"),
        P("col"),
        P("col"),
        P("col", "row"),
    )
    return jax.shard_map(
        layer,
        mesh=mesh,
        in_specs=placed,
        out_specs=(
            P("col", "row"),
            P("col", "row"),
            P("row", "col"),
            P("row", "col"),
            P("row", "col"),
            P("col"),
            P("col"),
            P("col", "row"),
            P("col"),
            P("col"),
            P("col"),
            P("row", "col"),
            P("col"),
            P("col", "row"),
            P("col"),
            P("col"),
            P("col"),
        ),
        check_vma=False,
    )
```

```python
from functools import partial
import functools

import jax
import jax.numpy as jnp
from jax import lax
from jax.experimental import pallas as pl
from jax.experimental.pallas import tpu as pltpu
from jax.sharding import PartitionSpec as P

D = 768
HEADS = 12
BQ = 256


def _mask(lab_q, lab_k, q0, bq, nk):
    rows = q0 + lax.broadcasted_iota(jnp.int32, (bq, nk), 0)
    cols = lax.broadcasted_iota(jnp.int32, (bq, nk), 1)
    return ((lab_q == lab_k) & (lab_k > 0)) | (rows == cols)


def _fwd_kernel(scale, q_ref, k_ref, v_ref, lq_ref, lk_ref, o_ref, m_ref, l_ref):
    i = pl.program_id(1)
    bq = q_ref.shape[0]
    nk = k_ref.shape[0]
    s = lax.dot_general(q_ref[...], k_ref[...], (((1,), (1,)), ((), ())),
                        preferred_element_type=jnp.float32) * scale
    allowed = _mask(lq_ref[...], lk_ref[...], i * bq, bq, nk)
    s = jnp.where(allowed, s, -1000000000.0)
    m = jnp.max(s, axis=1, keepdims=True)
    e = jnp.exp(s - m)
    l = jnp.sum(e, axis=1, keepdims=True)
    p = (e / l).astype(jnp.bfloat16)
    o_ref[...] = jnp.dot(p, v_ref[...], preferred_element_type=jnp.float32).astype(o_ref.dtype)
    m_ref[...] = m
    l_ref[...] = l


def _bwd_kernel(scale, q_ref, k_ref, v_ref, do_ref, lq_ref, lk_ref, m_ref, l_ref,
                dq_ref, dk_ref, dv_ref):
    i = pl.program_id(1)
    bq = q_ref.shape[0]
    nk = k_ref.shape[0]

    @pl.when(i == 0)
    def _():
        dk_ref[...] = jnp.zeros_like(dk_ref)
        dv_ref[...] = jnp.zeros_like(dv_ref)

    q = q_ref[...]
    k = k_ref[...]
    s = lax.dot_general(q, k, (((1,), (1,)), ((), ())),
                        preferred_element_type=jnp.float32) * scale
    allowed = _mask(lq_ref[...], lk_ref[...], i * bq, bq, nk)
    s = jnp.where(allowed, s, -1000000000.0)
    p = jnp.where(allowed, jnp.exp(s - m_ref[...]) / l_ref[...], 0.0)
    do = do_ref[...]
    dp = lax.dot_general(do, v_ref[...], (((1,), (1,)), ((), ())),
                         preferred_element_type=jnp.float32)
    inner = jnp.sum(p * dp, axis=1, keepdims=True)
    ds = (p * (dp - inner)).astype(jnp.bfloat16)
    dq_ref[...] = (jnp.dot(ds, k, preferred_element_type=jnp.float32) * scale).astype(dq_ref.dtype)
    dk_ref[...] += lax.dot_general(ds, q, (((0,), (0,)), ((), ())),
                                   preferred_element_type=jnp.float32) * scale
    dv_ref[...] += lax.dot_general(p.astype(jnp.bfloat16), do, (((0,), (0,)), ((), ())),
                                   preferred_element_type=jnp.float32)


def attention_forward(q, k, v, labels, scale):
    nh, seq, hd = q.shape
    bq = min(BQ, seq)
    lq = labels.reshape(seq, 1)
    lk = labels.reshape(1, seq)
    grid = (nh, seq // bq)
    qspec = pl.BlockSpec((None, bq, hd), lambda h, i: (h, i, 0))
    kspec = pl.BlockSpec((None, seq, hd), lambda h, i: (h, 0, 0))
    rowspec = pl.BlockSpec((None, bq, 1), lambda h, i: (h, i, 0))
    flops = 4 * nh * seq * seq * hd
    return pl.pallas_call(
        functools.partial(_fwd_kernel, scale),
        grid=grid,
        in_specs=[qspec, kspec, kspec,
                  pl.BlockSpec((bq, 1), lambda h, i: (i, 0)),
                  pl.BlockSpec((1, seq), lambda h, i: (0, 0))],
        out_specs=[qspec, rowspec, rowspec],
        out_shape=[jax.ShapeDtypeStruct((nh, seq, hd), jnp.bfloat16),
                   jax.ShapeDtypeStruct((nh, seq, 1), jnp.float32),
                   jax.ShapeDtypeStruct((nh, seq, 1), jnp.float32)],
        compiler_params=pltpu.CompilerParams(
            dimension_semantics=("parallel", "arbitrary"),
            vmem_limit_bytes=48 * 1024 * 1024),
        cost_estimate=pl.CostEstimate(flops=flops, transcendentals=nh * seq * seq,
                                      bytes_accessed=4 * nh * seq * hd * 2),
    )(q, k, v, lq, lk)


def attention_backward(q, k, v, do, labels, m, l, scale):
    nh, seq, hd = q.shape
    bq = min(BQ, seq)
    lq = labels.reshape(seq, 1)
    lk = labels.reshape(1, seq)
    grid = (nh, seq // bq)
    qspec = pl.BlockSpec((None, bq, hd), lambda h, i: (h, i, 0))
    kspec = pl.BlockSpec((None, seq, hd), lambda h, i: (h, 0, 0))
    rowspec = pl.BlockSpec((None, bq, 1), lambda h, i: (h, i, 0))
    flops = 10 * nh * seq * seq * hd
    return pl.pallas_call(
        functools.partial(_bwd_kernel, scale),
        grid=grid,
        in_specs=[qspec, kspec, kspec, qspec,
                  pl.BlockSpec((bq, 1), lambda h, i: (i, 0)),
                  pl.BlockSpec((1, seq), lambda h, i: (0, 0)),
                  rowspec, rowspec],
        out_specs=[qspec, kspec, kspec],
        out_shape=[jax.ShapeDtypeStruct((nh, seq, hd), jnp.bfloat16),
                   jax.ShapeDtypeStruct((nh, seq, hd), jnp.float32),
                   jax.ShapeDtypeStruct((nh, seq, hd), jnp.float32)],
        compiler_params=pltpu.CompilerParams(
            dimension_semantics=("parallel", "arbitrary"),
            vmem_limit_bytes=48 * 1024 * 1024),
        cost_estimate=pl.CostEstimate(flops=flops, transcendentals=nh * seq * seq,
                                      bytes_accessed=8 * nh * seq * hd * 2),
    )(q, k, v, do, lq, lk, m, l)


NORM_EPS = 1e-06


def feature_whole(blocked):
    return lax.all_gather(blocked, "col", axis=1, tiled=True)


def feature_sum(partial_rows):
    return lax.psum_scatter(
        partial_rows.astype(jnp.bfloat16), "col", scatter_dimension=1, tiled=True
    ).astype(jnp.float32)


def row_totals(first_term, second_term):
    return lax.psum((jnp.sum(first_term, axis=1), jnp.sum(second_term, axis=1)), "col")


def norm_forward(row_values, gain_row, shift_row):
    totals, squares = row_totals(row_values, row_values * row_values)
    mean_row = (totals / D)[:, None]
    var_row = (squares / D)[:, None] - mean_row * mean_row
    inverse = lax.rsqrt(var_row + NORM_EPS)
    normed = (row_values - mean_row) * inverse
    return (normed * gain_row + shift_row, normed, inverse)


def norm_backward(grad_rows, normed, inverse, gain_row):
    scaled = grad_rows * gain_row
    totals, along = row_totals(scaled, scaled * normed)
    back_rows = inverse * (scaled - (totals / D)[:, None] - normed * (along / D)[:, None])
    return (back_rows, jnp.sum(grad_rows * normed, axis=0), jnp.sum(grad_rows, axis=0))


def row_scatter_sum(partial_rows):
    count = lax.axis_size("row")
    me = lax.axis_index("row")
    blocks = partial_rows.reshape((count, partial_rows.shape[0] // count) + partial_rows.shape[1:])
    total = blocks[me]
    for shift in range(1, count):
        outgoing = blocks[lax.rem(me + shift, count)]
        total = total + lax.ppermute(
            outgoing, "row", [(i, (i + shift) % count) for i in range(count)]
        )
    return total


def row_sum(values):
    count = lax.axis_size("row")
    total = values
    for shift in range(1, count):
        total = total + lax.ppermute(
            values, "row", [(i, (i + shift) % count) for i in range(count)]
        )
    return total


def axis_gather(values, axis):
    count = lax.axis_size(axis)
    me = lax.axis_index(axis)
    arrived = [values]
    for shift in range(1, count):
        arrived.append(
            lax.ppermute(values, axis, [(i, (i + shift) % count) for i in range(count)])
        )
    order = lax.rem(me - jnp.arange(count) + count, count)
    return jnp.stack(arrived)[order]


def weight_partial(gathered, local_grad):
    return lax.dot_general(
        gathered, local_grad, (((0,), (0,)), ((), ())), preferred_element_type=jnp.float32
    )


def rows_gathered_many(blocks_and_axes, sent=False):
    flat = jnp.concatenate([block.reshape(-1) for block, _ in blocks_and_axes])
    if sent:
        pieces = axis_gather(flat, "row")
    else:
        pieces = lax.all_gather(flat, "row", axis=0, tiled=False)
    wholes = []
    offset = 0
    for block, axis in blocks_and_axes:
        piece = pieces[:, offset : offset + block.size].reshape((-1,) + block.shape)
        offset += block.size
        piece = jnp.moveaxis(piece, 0, axis)
        shape = list(block.shape)
        shape[axis] = shape[axis] * piece.shape[axis]
        wholes.append(piece.reshape(shape))
    return wholes


def heads_major(rows, head_size):
    return rows.reshape(rows.shape[0], -1, head_size).transpose(1, 0, 2)


def heads_beside(stacked):
    return stacked.transpose(1, 0, 2).reshape(stacked.shape[1], -1)


def full_norm(row_values, gain_full, shift_full):
    mean_row = jnp.sum(row_values, axis=1, keepdims=True) / D
    var_row = jnp.sum(row_values * row_values, axis=1, keepdims=True) / D - mean_row * mean_row
    inverse = lax.rsqrt(var_row + NORM_EPS)
    normed = (row_values - mean_row) * inverse
    return (normed * gain_full + shift_full, normed, inverse)


def layer(
    inputs,
    segments,
    query_weight,
    key_weight,
    value_weight,
    query_bias,
    value_bias,
    output_weight,
    output_bias,
    attn_gain,
    attn_shift,
    up_weight,
    up_bias,
    down_weight,
    down_bias,
    final_gain,
    final_shift,
    cotangent,
):
    head_size = D // HEADS
    score_scale = head_size ** (-0.5)
    labels = segments[0]
    token_rows = inputs.T
    out_grad = cotangent.T.astype(jnp.float32)
    own_features = token_rows.shape[1]
    own_start = lax.axis_index("col") * own_features
    inputs_full = axis_gather(inputs, "col").reshape(-1, inputs.shape[1]).T
    qkv_stack = jnp.stack([query_weight, key_weight, value_weight])
    qkv_complete, output_rows = rows_gathered_many(((qkv_stack, 1), (output_weight, 1)), sent=True)
    output_complete = lax.all_gather(output_rows, "col", axis=0, tiled=True)
    up_complete, down_complete = rows_gathered_many(((up_weight, 0), (down_weight, 1)))
    projected = jnp.einsum(
        "td,kdc->ktc", inputs_full, qkv_complete, preferred_element_type=jnp.float32
    )
    queries = heads_major((projected[0] + query_bias).astype(jnp.bfloat16), head_size)
    key_all = heads_major(projected[1].astype(jnp.bfloat16), head_size)
    value_all = heads_major((projected[2] + value_bias).astype(jnp.bfloat16), head_size)
    attended_h, row_max, row_total = attention_forward(
        queries, key_all, value_all, labels, score_scale
    )
    attended = heads_beside(attended_h)
    attended_full = feature_whole(attended)
    vectors_full = axis_gather(jnp.stack([output_bias, attn_gain, attn_shift]), "col")
    output_bias_full, gain_one_full, shift_one_full = (
        vectors_full[:, which].reshape(-1) for which in range(3)
    )
    first_sum_full = (
        inputs_full.astype(jnp.float32)
        + jnp.dot(attended_full, output_complete, preferred_element_type=jnp.float32)
        + output_bias_full
    )
    hidden_full_f, normed_one_full, inverse_one = full_norm(
        first_sum_full, gain_one_full, shift_one_full
    )
    hidden = lax.dynamic_slice_in_dim(hidden_full_f, own_start, own_features, axis=1)
    normed_one = lax.dynamic_slice_in_dim(normed_one_full, own_start, own_features, axis=1)
    hidden_full = hidden_full_f.astype(jnp.bfloat16)
    upped = jnp.dot(hidden_full, up_complete, preferred_element_type=jnp.float32) + up_bias
    acted_f, gelu_pull = jax.vjp(partial(jax.nn.gelu, approximate=False), upped)
    acted = acted_f.astype(jnp.bfloat16)
    ffn_partial = jnp.dot(acted, down_complete, preferred_element_type=jnp.float32)
    second_sum = hidden + feature_sum(ffn_partial) + down_bias
    result, normed_two, inverse_two = norm_forward(second_sum, final_gain, final_shift)
    second_grad, final_gain_grad, final_shift_grad = norm_backward(
        out_grad, normed_two, inverse_two, final_gain
    )
    branch_grad = second_grad.astype(jnp.bfloat16)
    branch_full = feature_whole(branch_grad)
    down_partial = weight_partial(branch_full, acted)
    acted_grad = lax.dot_general(
        branch_full, down_complete, (((1,), (1,)), ((), ())), preferred_element_type=jnp.float32
    )
    upped_grad = gelu_pull(acted_grad)[0].astype(jnp.bfloat16)
    up_partial = weight_partial(hidden_full, upped_grad)
    hidden_grad = second_grad + feature_sum(
        lax.dot_general(
            upped_grad, up_complete, (((1,), (1,)), ((), ())), preferred_element_type=jnp.float32
        )
    )
    first_grad, attn_gain_grad, attn_shift_grad = norm_backward(
        hidden_grad, normed_one, inverse_one, attn_gain
    )
    attn_branch_grad = first_grad.astype(jnp.bfloat16)
    attn_branch_full = feature_whole(attn_branch_grad)
    output_partial = weight_partial(attn_branch_full, attended)
    early_grads = row_scatter_sum(
        jnp.concatenate([down_partial, up_partial, output_partial], axis=1)
    )
    down_end = down_partial.shape[1]
    up_end = down_end + up_partial.shape[1]
    down_weight_grad = early_grads[:, :down_end].T
    up_weight_grad = early_grads[:, down_end:up_end]
    output_weight_grad = early_grads[:, up_end:].T
    attended_grad = lax.dot_general(
        attn_branch_full, output_rows, (((1,), (1,)), ((), ())), preferred_element_type=jnp.float32
    ).astype(jnp.bfloat16)
    query_grad_h, key_grad_h, value_grad_h = attention_backward(
        queries,
        key_all,
        value_all,
        heads_major(attended_grad, head_size),
        labels,
        row_max,
        row_total,
        score_scale,
    )
    query_grad = heads_beside(query_grad_h)
    key_grad = heads_beside(key_grad_h).astype(jnp.bfloat16)
    value_grad = heads_beside(value_grad_h).astype(jnp.bfloat16)
    column_count = query_weight.shape[1]
    qkv_partial = weight_partial(
        inputs_full, jnp.concatenate([query_grad, key_grad, value_grad], axis=1)
    )
    input_grad = first_grad + feature_sum(
        jnp.einsum(
            "ktc,kdc->td",
            jnp.stack([query_grad, key_grad, value_grad]),
            qkv_complete,
            preferred_element_type=jnp.float32,
        )
    )
    param_parts = (
        jnp.sum(query_grad.astype(jnp.float32), axis=0),
        jnp.sum(value_grad.astype(jnp.float32), axis=0),
        jnp.sum(attn_branch_grad.astype(jnp.float32), axis=0),
        attn_gain_grad,
        attn_shift_grad,
        jnp.sum(upped_grad.astype(jnp.float32), axis=0),
        jnp.sum(branch_grad.astype(jnp.float32), axis=0),
        final_gain_grad,
        final_shift_grad,
    )
    param_flat = jnp.concatenate(param_parts)
    row_count = lax.axis_size("row")
    width = qkv_partial.shape[1]
    if param_flat.shape[0] % width == 0:
        extra_rows = param_flat.shape[0] // width
        blocks = qkv_partial.reshape(row_count, -1, width)
        extra = jnp.broadcast_to(
            param_flat.reshape(1, extra_rows, width), (row_count, extra_rows, width)
        )
        summed = row_scatter_sum(jnp.concatenate([blocks, extra], axis=1).reshape(-1, width))
        qkv_grads = summed[:-extra_rows]
        param_flat = summed[-extra_rows:].reshape(-1)
    else:
        qkv_grads = row_scatter_sum(qkv_partial)
        param_flat = row_sum(param_flat)
    param_totals = []
    offset = 0
    for part in param_parts:
        param_totals.append(param_flat[offset : offset + part.shape[0]])
        offset += part.shape[0]
    return (
        result.astype(jnp.bfloat16).T,
        input_grad.astype(jnp.bfloat16).T,
        qkv_grads[:, :column_count],
        qkv_grads[:, column_count : 2 * column_count],
        qkv_grads[:, 2 * column_count :],
        param_totals[0],
        param_totals[1],
        output_weight_grad,
        param_totals[2],
        param_totals[3],
        param_totals[4],
        up_weight_grad,
        param_totals[5],
        down_weight_grad,
        param_totals[6],
        param_totals[7],
        param_totals[8],
    )


def solution(mesh):
    placed = (
        P("col", "row"),
        P("row", None),
        P("row", "col"),
        P("row", "col"),
        P("row", "col"),
        P("col"),
        P("col"),
        P("col", "row"),
        P("col"),
        P("col"),
        P("col"),
        P("row", "col"),
        P("col"),
        P("col", "row"),
        P("col"),
        P("col"),
        P("col"),
        P("col", "row"),
    )
    return jax.shard_map(
        layer,
        mesh=mesh,
        in_specs=placed,
        out_specs=(
            P("col", "row"),
            P("col", "row"),
            P("row", "col"),
            P("row", "col"),
            P("row", "col"),
            P("col"),
            P("col"),
            P("col", "row"),
            P("col"),
            P("col"),
            P("col"),
            P("row", "col"),
            P("col"),
            P("col", "row"),
            P("col"),
            P("col"),
            P("col"),
        ),
        check_vma=False,
    )
```

```python
from functools import partial
import functools

import jax
import jax.numpy as jnp
from jax import lax
from jax.experimental import pallas as pl
from jax.experimental.pallas import tpu as pltpu
from jax.sharding import PartitionSpec as P

D = 768
HEADS = 12
BQ = 256


def _mask(lab_q, lab_k, q0, bq, nk):
    rows = q0 + lax.broadcasted_iota(jnp.int32, (bq, nk), 0)
    cols = lax.broadcasted_iota(jnp.int32, (bq, nk), 1)
    return ((lab_q == lab_k) & (lab_k > 0)) | (rows == cols)


def _fwd_kernel(scale, q_ref, k_ref, v_ref, lq_ref, lk_ref, o_ref, m_ref, l_ref):
    i = pl.program_id(1)
    bq = q_ref.shape[0]
    nk = k_ref.shape[0]
    s = lax.dot_general(q_ref[...], k_ref[...], (((1,), (1,)), ((), ())),
                        preferred_element_type=jnp.float32) * scale
    allowed = _mask(lq_ref[...], lk_ref[...], i * bq, bq, nk)
    s = jnp.where(allowed, s, -1000000000.0)
    m = jnp.max(s, axis=1, keepdims=True)
    e = jnp.exp(s - m)
    l = jnp.sum(e, axis=1, keepdims=True)
    p = (e / l).astype(jnp.bfloat16)
    o_ref[...] = jnp.dot(p, v_ref[...], preferred_element_type=jnp.float32).astype(o_ref.dtype)
    m_ref[...] = m
    l_ref[...] = l


def _bwd_kernel(scale, q_ref, k_ref, v_ref, do_ref, lq_ref, lk_ref, m_ref, l_ref,
                dq_ref, dk_ref, dv_ref):
    i = pl.program_id(1)
    bq = q_ref.shape[0]
    nk = k_ref.shape[0]

    @pl.when(i == 0)
    def _():
        dk_ref[...] = jnp.zeros_like(dk_ref)
        dv_ref[...] = jnp.zeros_like(dv_ref)

    q = q_ref[...]
    k = k_ref[...]
    s = lax.dot_general(q, k, (((1,), (1,)), ((), ())),
                        preferred_element_type=jnp.float32) * scale
    allowed = _mask(lq_ref[...], lk_ref[...], i * bq, bq, nk)
    s = jnp.where(allowed, s, -1000000000.0)
    p = jnp.where(allowed, jnp.exp(s - m_ref[...]) / l_ref[...], 0.0)
    do = do_ref[...]
    dp = lax.dot_general(do, v_ref[...], (((1,), (1,)), ((), ())),
                         preferred_element_type=jnp.float32)
    inner = jnp.sum(p * dp, axis=1, keepdims=True)
    ds = (p * (dp - inner)).astype(jnp.bfloat16)
    dq_ref[...] = (jnp.dot(ds, k, preferred_element_type=jnp.float32) * scale).astype(dq_ref.dtype)
    dk_ref[...] += lax.dot_general(ds, q, (((0,), (0,)), ((), ())),
                                   preferred_element_type=jnp.float32) * scale
    dv_ref[...] += lax.dot_general(p.astype(jnp.bfloat16), do, (((0,), (0,)), ((), ())),
                                   preferred_element_type=jnp.float32)


def attention_forward(q, k, v, labels, scale):
    nh, seq, hd = q.shape
    bq = min(BQ, seq)
    lq = labels.reshape(seq, 1)
    lk = labels.reshape(1, seq)
    grid = (nh, seq // bq)
    qspec = pl.BlockSpec((None, bq, hd), lambda h, i: (h, i, 0))
    kspec = pl.BlockSpec((None, seq, hd), lambda h, i: (h, 0, 0))
    rowspec = pl.BlockSpec((None, bq, 1), lambda h, i: (h, i, 0))
    flops = 4 * nh * seq * seq * hd
    return pl.pallas_call(
        functools.partial(_fwd_kernel, scale),
        grid=grid,
        in_specs=[qspec, kspec, kspec,
                  pl.BlockSpec((bq, 1), lambda h, i: (i, 0)),
                  pl.BlockSpec((1, seq), lambda h, i: (0, 0))],
        out_specs=[qspec, rowspec, rowspec],
        out_shape=[jax.ShapeDtypeStruct((nh, seq, hd), jnp.bfloat16),
                   jax.ShapeDtypeStruct((nh, seq, 1), jnp.float32),
                   jax.ShapeDtypeStruct((nh, seq, 1), jnp.float32)],
        compiler_params=pltpu.CompilerParams(
            dimension_semantics=("parallel", "arbitrary"),
            vmem_limit_bytes=48 * 1024 * 1024),
        cost_estimate=pl.CostEstimate(flops=flops, transcendentals=nh * seq * seq,
                                      bytes_accessed=4 * nh * seq * hd * 2),
    )(q, k, v, lq, lk)


def attention_backward(q, k, v, do, labels, m, l, scale):
    nh, seq, hd = q.shape
    bq = min(BQ, seq)
    lq = labels.reshape(seq, 1)
    lk = labels.reshape(1, seq)
    grid = (nh, seq // bq)
    qspec = pl.BlockSpec((None, bq, hd), lambda h, i: (h, i, 0))
    kspec = pl.BlockSpec((None, seq, hd), lambda h, i: (h, 0, 0))
    rowspec = pl.BlockSpec((None, bq, 1), lambda h, i: (h, i, 0))
    flops = 10 * nh * seq * seq * hd
    return pl.pallas_call(
        functools.partial(_bwd_kernel, scale),
        grid=grid,
        in_specs=[qspec, kspec, kspec, qspec,
                  pl.BlockSpec((bq, 1), lambda h, i: (i, 0)),
                  pl.BlockSpec((1, seq), lambda h, i: (0, 0)),
                  rowspec, rowspec],
        out_specs=[qspec, kspec, kspec],
        out_shape=[jax.ShapeDtypeStruct((nh, seq, hd), jnp.bfloat16),
                   jax.ShapeDtypeStruct((nh, seq, hd), jnp.float32),
                   jax.ShapeDtypeStruct((nh, seq, hd), jnp.float32)],
        compiler_params=pltpu.CompilerParams(
            dimension_semantics=("parallel", "arbitrary"),
            vmem_limit_bytes=48 * 1024 * 1024),
        cost_estimate=pl.CostEstimate(flops=flops, transcendentals=nh * seq * seq,
                                      bytes_accessed=8 * nh * seq * hd * 2),
    )(q, k, v, do, lq, lk, m, l)


NORM_EPS = 1e-06


def feature_whole(blocked):
    return lax.all_gather(blocked, "col", axis=1, tiled=True)


def feature_sum(partial_rows):
    return lax.psum_scatter(
        partial_rows.astype(jnp.bfloat16), "col", scatter_dimension=1, tiled=True
    ).astype(jnp.float32)


def row_totals(first_term, second_term):
    return lax.psum((jnp.sum(first_term, axis=1), jnp.sum(second_term, axis=1)), "col")


def norm_both(row_values, gain_row, shift_row, grad_rows):
    scaled = grad_rows * gain_row
    totals, squares, grad_totals, grad_along = lax.psum(
        jnp.stack(
            [
                jnp.sum(row_values, axis=1),
                jnp.sum(row_values * row_values, axis=1),
                jnp.sum(scaled, axis=1),
                jnp.sum(scaled * row_values, axis=1),
            ]
        ),
        "col",
    )
    mean_row = (totals / D)[:, None]
    var_row = (squares / D)[:, None] - mean_row * mean_row
    inverse = lax.rsqrt(var_row + NORM_EPS)
    normed = (row_values - mean_row) * inverse
    along = inverse * (grad_along[:, None] - mean_row * grad_totals[:, None])
    back_rows = inverse * (scaled - (grad_totals / D)[:, None] - normed * (along / D))
    return (
        normed * gain_row + shift_row,
        back_rows,
        jnp.sum(grad_rows * normed, axis=0),
        jnp.sum(grad_rows, axis=0),
    )


def norm_backward(grad_rows, normed, inverse, gain_row):
    scaled = grad_rows * gain_row
    totals, along = row_totals(scaled, scaled * normed)
    back_rows = inverse * (scaled - (totals / D)[:, None] - normed * (along / D)[:, None])
    return (back_rows, jnp.sum(grad_rows * normed, axis=0), jnp.sum(grad_rows, axis=0))


def row_scatter_sum(partial_rows):
    count = lax.axis_size("row")
    me = lax.axis_index("row")
    blocks = partial_rows.reshape((count, partial_rows.shape[0] // count) + partial_rows.shape[1:])
    total = blocks[me]
    for shift in range(1, count):
        outgoing = blocks[lax.rem(me + shift, count)]
        total = total + lax.ppermute(
            outgoing, "row", [(i, (i + shift) % count) for i in range(count)]
        )
    return total


def row_sum(values):
    count = lax.axis_size("row")
    total = values
    for shift in range(1, count):
        total = total + lax.ppermute(
            values, "row", [(i, (i + shift) % count) for i in range(count)]
        )
    return total


def axis_gather(values, axis):
    count = lax.axis_size(axis)
    me = lax.axis_index(axis)
    arrived = [values]
    for shift in range(1, count):
        arrived.append(
            lax.ppermute(values, axis, [(i, (i + shift) % count) for i in range(count)])
        )
    order = lax.rem(me - jnp.arange(count) + count, count)
    return jnp.stack(arrived)[order]


def weight_partial(gathered, local_grad):
    return lax.dot_general(
        gathered, local_grad, (((0,), (0,)), ((), ())), preferred_element_type=jnp.float32
    )


def weight_grad(gathered, local_grad):
    return row_scatter_sum(
        lax.dot_general(
            gathered, local_grad, (((0,), (0,)), ((), ())), preferred_element_type=jnp.float32
        )
    )


def rows_gathered_many(blocks_and_axes, sent=False):
    flat = jnp.concatenate([block.reshape(-1) for block, _ in blocks_and_axes])
    if sent:
        pieces = axis_gather(flat, "row")
    else:
        pieces = lax.all_gather(flat, "row", axis=0, tiled=False)
    wholes = []
    offset = 0
    for block, axis in blocks_and_axes:
        piece = pieces[:, offset : offset + block.size].reshape((-1,) + block.shape)
        offset += block.size
        piece = jnp.moveaxis(piece, 0, axis)
        shape = list(block.shape)
        shape[axis] = shape[axis] * piece.shape[axis]
        wholes.append(piece.reshape(shape))
    return wholes


def heads_major(rows, head_size):
    return rows.reshape(rows.shape[0], -1, head_size).transpose(1, 0, 2)


def heads_beside(stacked):
    return stacked.transpose(1, 0, 2).reshape(stacked.shape[1], -1)


def full_norm(row_values, gain_full, shift_full):
    mean_row = jnp.sum(row_values, axis=1, keepdims=True) / D
    var_row = jnp.sum(row_values * row_values, axis=1, keepdims=True) / D - mean_row * mean_row
    inverse = lax.rsqrt(var_row + NORM_EPS)
    normed = (row_values - mean_row) * inverse
    return (normed * gain_full + shift_full, normed, inverse)


def layer(
    inputs,
    segments,
    query_weight,
    key_weight,
    value_weight,
    query_bias,
    value_bias,
    output_weight,
    output_bias,
    attn_gain,
    attn_shift,
    up_weight,
    up_bias,
    down_weight,
    down_bias,
    final_gain,
    final_shift,
    cotangent,
):
    head_size = D // HEADS
    score_scale = head_size ** (-0.5)
    labels = segments[0]
    token_rows = inputs.T
    out_grad = cotangent.T.astype(jnp.float32)
    own_features = token_rows.shape[1]
    own_start = lax.axis_index("col") * own_features
    inputs_full = axis_gather(inputs, "col").reshape(-1, inputs.shape[1]).T
    qkv_stack = jnp.stack([query_weight, key_weight, value_weight])
    qkv_complete, output_rows = rows_gathered_many(((qkv_stack, 1), (output_weight, 1)), sent=True)
    output_complete = lax.all_gather(output_rows, "col", axis=0, tiled=True)
    up_complete, down_complete = rows_gathered_many(((up_weight, 0), (down_weight, 1)))
    projected = jnp.einsum(
        "td,kdc->ktc", inputs_full, qkv_complete, preferred_element_type=jnp.float32
    )
    queries = heads_major((projected[0] + query_bias).astype(jnp.bfloat16), head_size)
    key_all = heads_major(projected[1].astype(jnp.bfloat16), head_size)
    value_all = heads_major((projected[2] + value_bias).astype(jnp.bfloat16), head_size)
    attended_h, row_max, row_total = attention_forward(
        queries, key_all, value_all, labels, score_scale
    )
    attended = heads_beside(attended_h)
    attended_full = feature_whole(attended)
    vectors_full = axis_gather(jnp.stack([output_bias, attn_gain, attn_shift]), "col")
    output_bias_full, gain_one_full, shift_one_full = (
        vectors_full[:, which].reshape(-1) for which in range(3)
    )
    first_sum_full = (
        inputs_full.astype(jnp.float32)
        + jnp.dot(attended_full, output_complete, preferred_element_type=jnp.float32)
        + output_bias_full
    )
    hidden_full_f, normed_one_full, inverse_one = full_norm(
        first_sum_full, gain_one_full, shift_one_full
    )
    hidden = lax.dynamic_slice_in_dim(hidden_full_f, own_start, own_features, axis=1)
    normed_one = lax.dynamic_slice_in_dim(normed_one_full, own_start, own_features, axis=1)
    hidden_full = hidden_full_f.astype(jnp.bfloat16)
    upped = jnp.dot(hidden_full, up_complete, preferred_element_type=jnp.float32) + up_bias
    acted_f, gelu_pull = jax.vjp(partial(jax.nn.gelu, approximate=False), upped)
    acted = acted_f.astype(jnp.bfloat16)
    ffn_partial = jnp.dot(acted, down_complete, preferred_element_type=jnp.float32)
    second_sum = hidden + feature_sum(ffn_partial) + down_bias
    result, second_grad, final_gain_grad, final_shift_grad = norm_both(
        second_sum, final_gain, final_shift, out_grad
    )
    branch_grad = second_grad.astype(jnp.bfloat16)
    branch_full = feature_whole(branch_grad)
    down_partial = weight_partial(branch_full, acted)
    acted_grad = lax.dot_general(
        branch_full, down_complete, (((1,), (1,)), ((), ())), preferred_element_type=jnp.float32
    )
    upped_grad = gelu_pull(acted_grad)[0].astype(jnp.bfloat16)
    up_partial = weight_partial(hidden_full, upped_grad)
    ffn_grads = row_scatter_sum(jnp.concatenate([down_partial, up_partial], axis=1))
    down_weight_grad = ffn_grads[:, : down_partial.shape[1]].T
    up_weight_grad = ffn_grads[:, down_partial.shape[1] :]
    hidden_grad = second_grad + feature_sum(
        lax.dot_general(
            upped_grad, up_complete, (((1,), (1,)), ((), ())), preferred_element_type=jnp.float32
        )
    )
    first_grad, attn_gain_grad, attn_shift_grad = norm_backward(
        hidden_grad, normed_one, inverse_one, attn_gain
    )
    attn_branch_grad = first_grad.astype(jnp.bfloat16)
    attn_branch_full = feature_whole(attn_branch_grad)
    output_weight_grad = weight_grad(attn_branch_full, attended).T
    attended_grad = lax.dot_general(
        attn_branch_full, output_rows, (((1,), (1,)), ((), ())), preferred_element_type=jnp.float32
    ).astype(jnp.bfloat16)
    query_grad_h, key_grad_h, value_grad_h = attention_backward(
        queries,
        key_all,
        value_all,
        heads_major(attended_grad, head_size),
        labels,
        row_max,
        row_total,
        score_scale,
    )
    query_grad = heads_beside(query_grad_h)
    key_grad = heads_beside(key_grad_h).astype(jnp.bfloat16)
    value_grad = heads_beside(value_grad_h).astype(jnp.bfloat16)
    column_count = query_weight.shape[1]
    qkv_grads = weight_grad(
        inputs_full, jnp.concatenate([query_grad, key_grad, value_grad], axis=1)
    )
    input_grad = first_grad + feature_sum(
        jnp.einsum(
            "ktc,kdc->td",
            jnp.stack([query_grad, key_grad, value_grad]),
            qkv_complete,
            preferred_element_type=jnp.float32,
        )
    )
    param_parts = (
        jnp.sum(query_grad.astype(jnp.float32), axis=0),
        jnp.sum(value_grad.astype(jnp.float32), axis=0),
        jnp.sum(attn_branch_grad.astype(jnp.float32), axis=0),
        attn_gain_grad,
        attn_shift_grad,
        jnp.sum(upped_grad.astype(jnp.float32), axis=0),
        jnp.sum(branch_grad.astype(jnp.float32), axis=0),
        final_gain_grad,
        final_shift_grad,
    )
    param_flat = row_sum(jnp.concatenate(param_parts))
    param_totals = []
    offset = 0
    for part in param_parts:
        param_totals.append(param_flat[offset : offset + part.shape[0]])
        offset += part.shape[0]
    return (
        result.astype(jnp.bfloat16).T,
        input_grad.astype(jnp.bfloat16).T,
        qkv_grads[:, :column_count],
        qkv_grads[:, column_count : 2 * column_count],
        qkv_grads[:, 2 * column_count :],
        param_totals[0],
        param_totals[1],
        output_weight_grad,
        param_totals[2],
        param_totals[3],
        param_totals[4],
        up_weight_grad,
        param_totals[5],
        down_weight_grad,
        param_totals[6],
        param_totals[7],
        param_totals[8],
    )


def solution(mesh):
    placed = (
        P("col", "row"),
        P("row", None),
        P("row", "col"),
        P("row", "col"),
        P("row", "col"),
        P("col"),
        P("col"),
        P("col", "row"),
        P("col"),
        P("col"),
        P("col"),
        P("row", "col"),
        P("col"),
        P("col", "row"),
        P("col"),
        P("col"),
        P("col"),
        P("col", "row"),
    )
    return jax.shard_map(
        layer,
        mesh=mesh,
        in_specs=placed,
        out_specs=(
            P("col", "row"),
            P("col", "row"),
            P("row", "col"),
            P("row", "col"),
            P("row", "col"),
            P("col"),
            P("col"),
            P("col", "row"),
            P("col"),
            P("col"),
            P("col"),
            P("row", "col"),
            P("col"),
            P("col", "row"),
            P("col"),
            P("col"),
            P("col"),
        ),
        check_vma=False,
    )
```

```python
from functools import partial
import functools

import jax
import jax.numpy as jnp
from jax import lax
from jax.experimental import pallas as pl
from jax.experimental.pallas import tpu as pltpu
from jax.sharding import PartitionSpec as P

D = 768
HEADS = 12
BQ = 256


def _mask(lab_q, lab_k, q0, bq, nk):
    rows = q0 + lax.broadcasted_iota(jnp.int32, (bq, nk), 0)
    cols = lax.broadcasted_iota(jnp.int32, (bq, nk), 1)
    return ((lab_q == lab_k) & (lab_k > 0)) | (rows == cols)


def _fwd_kernel(scale, q_ref, k_ref, v_ref, lq_ref, lk_ref, o_ref, m_ref, l_ref):
    i = pl.program_id(1)
    bq = q_ref.shape[0]
    nk = k_ref.shape[0]
    s = lax.dot_general(q_ref[...], k_ref[...], (((1,), (1,)), ((), ())),
                        preferred_element_type=jnp.float32) * scale
    allowed = _mask(lq_ref[...], lk_ref[...], i * bq, bq, nk)
    s = jnp.where(allowed, s, -1000000000.0)
    m = jnp.max(s, axis=1, keepdims=True)
    e = jnp.exp(s - m)
    l = jnp.sum(e, axis=1, keepdims=True)
    p = (e / l).astype(jnp.bfloat16)
    o_ref[...] = jnp.dot(p, v_ref[...], preferred_element_type=jnp.float32).astype(o_ref.dtype)
    m_ref[...] = m
    l_ref[...] = l


def _bwd_kernel(scale, q_ref, k_ref, v_ref, do_ref, lq_ref, lk_ref, m_ref, l_ref,
                dq_ref, dk_ref, dv_ref):
    i = pl.program_id(1)
    bq = q_ref.shape[0]
    nk = k_ref.shape[0]

    @pl.when(i == 0)
    def _():
        dk_ref[...] = jnp.zeros_like(dk_ref)
        dv_ref[...] = jnp.zeros_like(dv_ref)

    q = q_ref[...]
    k = k_ref[...]
    s = lax.dot_general(q, k, (((1,), (1,)), ((), ())),
                        preferred_element_type=jnp.float32) * scale
    allowed = _mask(lq_ref[...], lk_ref[...], i * bq, bq, nk)
    s = jnp.where(allowed, s, -1000000000.0)
    p = jnp.where(allowed, jnp.exp(s - m_ref[...]) / l_ref[...], 0.0)
    do = do_ref[...]
    dp = lax.dot_general(do, v_ref[...], (((1,), (1,)), ((), ())),
                         preferred_element_type=jnp.float32)
    inner = jnp.sum(p * dp, axis=1, keepdims=True)
    ds = (p * (dp - inner)).astype(jnp.bfloat16)
    dq_ref[...] = (jnp.dot(ds, k, preferred_element_type=jnp.float32) * scale).astype(dq_ref.dtype)
    dk_ref[...] += lax.dot_general(ds, q, (((0,), (0,)), ((), ())),
                                   preferred_element_type=jnp.float32) * scale
    dv_ref[...] += lax.dot_general(p.astype(jnp.bfloat16), do, (((0,), (0,)), ((), ())),
                                   preferred_element_type=jnp.float32)


def attention_forward(q, k, v, labels, scale):
    nh, seq, hd = q.shape
    bq = min(BQ, seq)
    lq = labels.reshape(seq, 1)
    lk = labels.reshape(1, seq)
    grid = (nh, seq // bq)
    qspec = pl.BlockSpec((None, bq, hd), lambda h, i: (h, i, 0))
    kspec = pl.BlockSpec((None, seq, hd), lambda h, i: (h, 0, 0))
    rowspec = pl.BlockSpec((None, bq, 1), lambda h, i: (h, i, 0))
    flops = 4 * nh * seq * seq * hd
    return pl.pallas_call(
        functools.partial(_fwd_kernel, scale),
        grid=grid,
        in_specs=[qspec, kspec, kspec,
                  pl.BlockSpec((bq, 1), lambda h, i: (i, 0)),
                  pl.BlockSpec((1, seq), lambda h, i: (0, 0))],
        out_specs=[qspec, rowspec, rowspec],
        out_shape=[jax.ShapeDtypeStruct((nh, seq, hd), jnp.bfloat16),
                   jax.ShapeDtypeStruct((nh, seq, 1), jnp.float32),
                   jax.ShapeDtypeStruct((nh, seq, 1), jnp.float32)],
        compiler_params=pltpu.CompilerParams(
            dimension_semantics=("parallel", "arbitrary"),
            vmem_limit_bytes=48 * 1024 * 1024),
        cost_estimate=pl.CostEstimate(flops=flops, transcendentals=nh * seq * seq,
                                      bytes_accessed=4 * nh * seq * hd * 2),
    )(q, k, v, lq, lk)


def attention_backward(q, k, v, do, labels, m, l, scale):
    nh, seq, hd = q.shape
    bq = min(BQ, seq)
    lq = labels.reshape(seq, 1)
    lk = labels.reshape(1, seq)
    grid = (nh, seq // bq)
    qspec = pl.BlockSpec((None, bq, hd), lambda h, i: (h, i, 0))
    kspec = pl.BlockSpec((None, seq, hd), lambda h, i: (h, 0, 0))
    rowspec = pl.BlockSpec((None, bq, 1), lambda h, i: (h, i, 0))
    flops = 10 * nh * seq * seq * hd
    return pl.pallas_call(
        functools.partial(_bwd_kernel, scale),
        grid=grid,
        in_specs=[qspec, kspec, kspec, qspec,
                  pl.BlockSpec((bq, 1), lambda h, i: (i, 0)),
                  pl.BlockSpec((1, seq), lambda h, i: (0, 0)),
                  rowspec, rowspec],
        out_specs=[qspec, kspec, kspec],
        out_shape=[jax.ShapeDtypeStruct((nh, seq, hd), jnp.bfloat16),
                   jax.ShapeDtypeStruct((nh, seq, hd), jnp.float32),
                   jax.ShapeDtypeStruct((nh, seq, hd), jnp.float32)],
        compiler_params=pltpu.CompilerParams(
            dimension_semantics=("parallel", "arbitrary"),
            vmem_limit_bytes=48 * 1024 * 1024),
        cost_estimate=pl.CostEstimate(flops=flops, transcendentals=nh * seq * seq,
                                      bytes_accessed=8 * nh * seq * hd * 2),
    )(q, k, v, do, lq, lk, m, l)


NORM_EPS = 1e-06


def feature_whole(blocked):
    return lax.all_gather(blocked, "col", axis=1, tiled=True)


def feature_sum(partial_rows):
    return lax.psum_scatter(
        partial_rows.astype(jnp.bfloat16), "col", scatter_dimension=1, tiled=True
    ).astype(jnp.float32)


def row_totals(first_term, second_term):
    return lax.psum((jnp.sum(first_term, axis=1), jnp.sum(second_term, axis=1)), "col")


def norm_both(row_values, gain_row, shift_row, grad_rows):
    scaled = grad_rows * gain_row
    totals, squares, grad_totals, grad_along = lax.psum(
        jnp.stack(
            [
                jnp.sum(row_values, axis=1),
                jnp.sum(row_values * row_values, axis=1),
                jnp.sum(scaled, axis=1),
                jnp.sum(scaled * row_values, axis=1),
            ]
        ),
        "col",
    )
    mean_row = (totals / D)[:, None]
    var_row = (squares / D)[:, None] - mean_row * mean_row
    inverse = lax.rsqrt(var_row + NORM_EPS)
    normed = (row_values - mean_row) * inverse
    along = inverse * (grad_along[:, None] - mean_row * grad_totals[:, None])
    back_rows = inverse * (scaled - (grad_totals / D)[:, None] - normed * (along / D))
    return (
        normed * gain_row + shift_row,
        back_rows,
        jnp.sum(grad_rows * normed, axis=0),
        jnp.sum(grad_rows, axis=0),
    )


def norm_backward(grad_rows, normed, inverse, gain_row):
    scaled = grad_rows * gain_row
    totals, along = row_totals(scaled, scaled * normed)
    back_rows = inverse * (scaled - (totals / D)[:, None] - normed * (along / D)[:, None])
    return (back_rows, jnp.sum(grad_rows * normed, axis=0), jnp.sum(grad_rows, axis=0))


def row_scatter_sum(partial_rows):
    count = lax.axis_size("row")
    me = lax.axis_index("row")
    blocks = partial_rows.reshape((count, partial_rows.shape[0] // count) + partial_rows.shape[1:])
    total = blocks[me]
    for shift in range(1, count):
        outgoing = blocks[lax.rem(me + shift, count)]
        total = total + lax.ppermute(
            outgoing, "row", [(i, (i + shift) % count) for i in range(count)]
        )
    return total


def row_sum(values):
    count = lax.axis_size("row")
    if count & (count - 1):
        total = values
        for shift in range(1, count):
            total = total + lax.ppermute(
                values, "row", [(i, (i + shift) % count) for i in range(count)]
            )
        return total
    total = values
    bit = count // 2
    while bit >= 1:
        total = total + lax.ppermute(total, "row", [(i, i ^ bit) for i in range(count)])
        bit //= 2
    return total


def row_scatter_halving(partial_rows):
    count = lax.axis_size("row")
    if count & (count - 1):
        return row_scatter_sum(partial_rows)
    me = lax.axis_index("row")
    held = partial_rows.reshape((count, partial_rows.shape[0] // count) + partial_rows.shape[1:])
    bit = count // 2
    while bit >= 1:
        side = lax.rem(me // bit, 2)
        half = held.shape[0] // 2
        keep = lax.dynamic_slice_in_dim(held, side * half, half, axis=0)
        away = lax.dynamic_slice_in_dim(held, (1 - side) * half, half, axis=0)
        held = keep + lax.ppermute(away, "row", [(i, i ^ bit) for i in range(count)])
        bit //= 2
    return held[0]


def axis_gather(values, axis):
    count = lax.axis_size(axis)
    me = lax.axis_index(axis)
    arrived = [values]
    for shift in range(1, count):
        arrived.append(
            lax.ppermute(values, axis, [(i, (i + shift) % count) for i in range(count)])
        )
    order = lax.rem(me - jnp.arange(count) + count, count)
    return jnp.stack(arrived)[order]


def weight_partial(gathered, local_grad):
    return lax.dot_general(
        gathered, local_grad, (((0,), (0,)), ((), ())), preferred_element_type=jnp.float32
    )


def rows_gathered_many(blocks_and_axes, sent=False):
    flat = jnp.concatenate([block.reshape(-1) for block, _ in blocks_and_axes])
    if sent:
        pieces = axis_gather(flat, "row")
    else:
        pieces = lax.all_gather(flat, "row", axis=0, tiled=False)
    wholes = []
    offset = 0
    for block, axis in blocks_and_axes:
        piece = pieces[:, offset : offset + block.size].reshape((-1,) + block.shape)
        offset += block.size
        piece = jnp.moveaxis(piece, 0, axis)
        shape = list(block.shape)
        shape[axis] = shape[axis] * piece.shape[axis]
        wholes.append(piece.reshape(shape))
    return wholes


def heads_major(rows, head_size):
    return rows.reshape(rows.shape[0], -1, head_size).transpose(1, 0, 2)


def heads_beside(stacked):
    return stacked.transpose(1, 0, 2).reshape(stacked.shape[1], -1)


def full_norm(row_values, gain_full, shift_full):
    mean_row = jnp.sum(row_values, axis=1, keepdims=True) / D
    var_row = jnp.sum(row_values * row_values, axis=1, keepdims=True) / D - mean_row * mean_row
    inverse = lax.rsqrt(var_row + NORM_EPS)
    normed = (row_values - mean_row) * inverse
    return (normed * gain_full + shift_full, normed, inverse)


def layer(
    inputs,
    segments,
    query_weight,
    key_weight,
    value_weight,
    query_bias,
    value_bias,
    output_weight,
    output_bias,
    attn_gain,
    attn_shift,
    up_weight,
    up_bias,
    down_weight,
    down_bias,
    final_gain,
    final_shift,
    cotangent,
):
    head_size = D // HEADS
    score_scale = head_size ** (-0.5)
    labels = segments[0]
    token_rows = inputs.T
    out_grad = cotangent.T.astype(jnp.float32)
    own_features = token_rows.shape[1]
    own_start = lax.axis_index("col") * own_features
    inputs_full = axis_gather(inputs, "col").reshape(-1, inputs.shape[1]).T
    qkv_stack = jnp.stack([query_weight, key_weight, value_weight])
    qkv_complete, output_rows = rows_gathered_many(((qkv_stack, 1), (output_weight, 1)), sent=True)
    output_complete = lax.all_gather(output_rows, "col", axis=0, tiled=True)
    up_complete, down_complete = rows_gathered_many(((up_weight, 0), (down_weight, 1)))
    projected = jnp.einsum(
        "td,kdc->ktc", inputs_full, qkv_complete, preferred_element_type=jnp.float32
    )
    queries = heads_major((projected[0] + query_bias).astype(jnp.bfloat16), head_size)
    key_all = heads_major(projected[1].astype(jnp.bfloat16), head_size)
    value_all = heads_major((projected[2] + value_bias).astype(jnp.bfloat16), head_size)
    attended_h, row_max, row_total = attention_forward(
        queries, key_all, value_all, labels, score_scale
    )
    attended = heads_beside(attended_h)
    attended_full = feature_whole(attended)
    vectors_full = axis_gather(jnp.stack([output_bias, attn_gain, attn_shift]), "col")
    output_bias_full, gain_one_full, shift_one_full = (
        vectors_full[:, which].reshape(-1) for which in range(3)
    )
    first_sum_full = (
        inputs_full.astype(jnp.float32)
        + jnp.dot(attended_full, output_complete, preferred_element_type=jnp.float32)
        + output_bias_full
    )
    hidden_full_f, normed_one_full, inverse_one = full_norm(
        first_sum_full, gain_one_full, shift_one_full
    )
    hidden = lax.dynamic_slice_in_dim(hidden_full_f, own_start, own_features, axis=1)
    normed_one = lax.dynamic_slice_in_dim(normed_one_full, own_start, own_features, axis=1)
    hidden_full = hidden_full_f.astype(jnp.bfloat16)
    upped = jnp.dot(hidden_full, up_complete, preferred_element_type=jnp.float32) + up_bias
    acted_f, gelu_pull = jax.vjp(partial(jax.nn.gelu, approximate=False), upped)
    acted = acted_f.astype(jnp.bfloat16)
    ffn_partial = jnp.dot(acted, down_complete, preferred_element_type=jnp.float32)
    second_sum = hidden + feature_sum(ffn_partial) + down_bias
    result, second_grad, final_gain_grad, final_shift_grad = norm_both(
        second_sum, final_gain, final_shift, out_grad
    )
    branch_grad = second_grad.astype(jnp.bfloat16)
    branch_full = feature_whole(branch_grad)
    down_partial = weight_partial(branch_full, acted)
    acted_grad = lax.dot_general(
        branch_full, down_complete, (((1,), (1,)), ((), ())), preferred_element_type=jnp.float32
    )
    upped_grad = gelu_pull(acted_grad)[0].astype(jnp.bfloat16)
    up_partial = weight_partial(hidden_full, upped_grad)
    ffn_grads = row_scatter_sum(jnp.concatenate([down_partial, up_partial], axis=1))
    down_weight_grad = ffn_grads[:, : down_partial.shape[1]].T
    up_weight_grad = ffn_grads[:, down_partial.shape[1] :]
    hidden_grad = second_grad + feature_sum(
        lax.dot_general(
            upped_grad, up_complete, (((1,), (1,)), ((), ())), preferred_element_type=jnp.float32
        )
    )
    first_grad, attn_gain_grad, attn_shift_grad = norm_backward(
        hidden_grad, normed_one, inverse_one, attn_gain
    )
    attn_branch_grad = first_grad.astype(jnp.bfloat16)
    attn_branch_full = feature_whole(attn_branch_grad)
    output_weight_grad = row_scatter_halving(weight_partial(attn_branch_full, attended)).T
    attended_grad = lax.dot_general(
        attn_branch_full, output_rows, (((1,), (1,)), ((), ())), preferred_element_type=jnp.float32
    ).astype(jnp.bfloat16)
    query_grad_h, key_grad_h, value_grad_h = attention_backward(
        queries,
        key_all,
        value_all,
        heads_major(attended_grad, head_size),
        labels,
        row_max,
        row_total,
        score_scale,
    )
    query_grad = heads_beside(query_grad_h)
    key_grad = heads_beside(key_grad_h).astype(jnp.bfloat16)
    value_grad = heads_beside(value_grad_h).astype(jnp.bfloat16)
    column_count = query_weight.shape[1]
    qkv_grads = row_scatter_halving(
        weight_partial(inputs_full, jnp.concatenate([query_grad, key_grad, value_grad], axis=1))
    )
    input_grad = first_grad + feature_sum(
        jnp.einsum(
            "ktc,kdc->td",
            jnp.stack([query_grad, key_grad, value_grad]),
            qkv_complete,
            preferred_element_type=jnp.float32,
        )
    )
    param_parts = (
        jnp.sum(query_grad.astype(jnp.float32), axis=0),
        jnp.sum(value_grad.astype(jnp.float32), axis=0),
        jnp.sum(attn_branch_grad.astype(jnp.float32), axis=0),
        attn_gain_grad,
        attn_shift_grad,
        jnp.sum(upped_grad.astype(jnp.float32), axis=0),
        jnp.sum(branch_grad.astype(jnp.float32), axis=0),
        final_gain_grad,
        final_shift_grad,
    )
    param_flat = row_sum(jnp.concatenate(param_parts))
    param_totals = []
    offset = 0
    for part in param_parts:
        param_totals.append(param_flat[offset : offset + part.shape[0]])
        offset += part.shape[0]
    return (
        result.astype(jnp.bfloat16).T,
        input_grad.astype(jnp.bfloat16).T,
        qkv_grads[:, :column_count],
        qkv_grads[:, column_count : 2 * column_count],
        qkv_grads[:, 2 * column_count :],
        param_totals[0],
        param_totals[1],
        output_weight_grad,
        param_totals[2],
        param_totals[3],
        param_totals[4],
        up_weight_grad,
        param_totals[5],
        down_weight_grad,
        param_totals[6],
        param_totals[7],
        param_totals[8],
    )


def solution(mesh):
    placed = (
        P("col", "row"),
        P("row", None),
        P("row", "col"),
        P("row", "col"),
        P("row", "col"),
        P("col"),
        P("col"),
        P("col", "row"),
        P("col"),
        P("col"),
        P("col"),
        P("row", "col"),
        P("col"),
        P("col", "row"),
        P("col"),
        P("col"),
        P("col"),
        P("col", "row"),
    )
    return jax.shard_map(
        layer,
        mesh=mesh,
        in_specs=placed,
        out_specs=(
            P("col", "row"),
            P("col", "row"),
            P("row", "col"),
            P("row", "col"),
            P("row", "col"),
            P("col"),
            P("col"),
            P("col", "row"),
            P("col"),
            P("col"),
            P("col"),
            P("row", "col"),
            P("col"),
            P("col", "row"),
            P("col"),
            P("col"),
            P("col"),
        ),
        check_vma=False,
    )
```
